128 devices in a mesh: tile: 64 (over z_hi, y, x, core), head: 2 (over z_lo).
Axes of the slice: x: 4, y: 4, z: 4 (z_hi: 2, z_lo: 2; z = z_hi * 2 + z_lo), core: 2. Of those that a mesh axis runs over, the one named last changes fastest.
Arguments:
- traces: bfloat16 [4096, 128, 128], P('tile'), may hold values from -6 to 6
- trace_mask: int32 [4096, 128], P('tile'), may hold values 0 or 1
- embed_voxel: bfloat16 [4096, 768], P(None, 'head'), may hold values from -0.125 to 0.125
- embed_mask: bfloat16 [256, 768], P(None, 'head'), may hold values from -0.5 to 0.5
- position: bfloat16 [512, 768], P(None, 'head'), may hold values from -3 to 3
- norm_gain: float32 [3, 768], replicated, may hold values from 0.5 to 1.5
- norm_bias: float32 [3, 768], replicated, may hold values from -2 to 2
- w_qkv: bfloat16 [1, 3, 768, 768], P(None, None, None, 'head'), may hold values from -8 to 8
- w_out: bfloat16 [1, 768, 768], P(None, 'head'), may hold values from -0.21875 to 0.21875
- w_up: bfloat16 [1, 768, 3072], P(None, None, 'head'), may hold values from -0.21875 to 0.21875
- w_down: bfloat16 [1, 3072, 768], P(None, 'head'), may hold values from -0.109375 to 0.109375
- w_decode: bfloat16 [768, 4096], P(None, 'head'), may hold values from -0.21875 to 0.21875
Outputs:
- reconstruction: bfloat16 [4096, 128, 128], P('tile')
The draws below stay inside these ranges and needn't reach their ends.
Inputs may be any that keep to these rules, and one draw needn't show every extreme that they name: `trace_mask`: 1 marks a recorded trace, 0 a missing one.
All inputs are finite; a program needn't handle non-finite values. No bound on the sum of `trace_mask` on one device may be relied on, other than what follows from the above.
Results may differ from the reference program's by a relative error of at most 0.019.
Values may be sent and summed in bfloat16 or wider, within the bound.
No kernel may reach another device: no remote copies, remote signals or barrier semaphores. Data moves between devices by JAX's collectives and lax.ppermute only.
A program may use at most 256 MiB of HBM per device.

```python
import jax
import jax.numpy as jnp
from jax import lax

D = 768
HEADS = 12
MLP = 3072
PATCH = 16
LAYERS = 1
WIN = 128
HEAD_DIM = 64
HALF = 64
TOK = 512
PV = 4096
NIL = 4096
N_TILE = 64
N_HEAD = 2


def draw_w_qkv(key, part):
    base = jax.random.normal(key, (LAYERS, 3, D, D), jnp.float32) * D ** (-0.5)
    return base.astype(jnp.bfloat16)


def touch_ends(result, own_key, low, largest):
    shape = result.shape
    spot = [jax.random.randint(jax.random.fold_in(own_key, axis), (), 0, shape[axis]) for axis in range(len(shape))]
    result = result.at[tuple(spot)].set(low)
    longest = shape.index(max(shape))
    spot[longest] = (spot[longest] + 1) % shape[longest]
    return result.at[tuple(spot)].set(largest)


def steps_of(own_key, extent, shards, least, largest):
    level, own = 1.0, jax.random.fold_in(own_key, 6)
    for dim, shards_of in shards:
        steps = jnp.exp(jax.random.uniform(jax.random.fold_in(own, dim), (shards_of,), jnp.float32, least / len(shards), largest / len(shards)))
        level = level * jnp.repeat(steps, extent[dim] // shards_of).reshape([-1 if axis == dim else 1 for axis in range(len(extent))])
    return level


def centred(stream_key, extent, scale, most, shards=(), kind=jnp.bfloat16):
    result = scale * jax.random.normal(stream_key, extent, jnp.float32)
    if shards:
        result = result * steps_of(stream_key, extent, shards, -0.22, 0.18)
    return jnp.clip(result, -most, most).astype(kind)


def setup_inputs(seed: int = 0) -> dict:
    arg_keys = jax.random.split(jax.random.key(seed), 13)
    traces = centred(arg_keys[0], (NIL, WIN, WIN), 1.0, 6.0, ((0, 64),))
    trace_mask = touch_ends((jax.random.randint(arg_keys[1], (NIL, WIN), 0, 2) < 1).astype(jnp.int32), jax.random.fold_in(arg_keys[1], 1), 0, 1)
    embed_voxel = centred(arg_keys[2], (PV, D), (PV // 2) ** -0.5, 0.125, ((1, 2),))
    embed_mask = centred(arg_keys[3], (PATCH * PATCH, D), (PATCH * PATCH // 2) ** -0.5, 0.5, ((1, 2),))
    position = centred(arg_keys[4], (TOK, D), 0.5, 3.0, ((1, 2),))
    norm_gain = jnp.clip(jax.random.uniform(arg_keys[5], (2 * LAYERS + 1, D), jnp.float32, 0.5, 1.5), 0.5, 1.5)
    norm_bias = centred(arg_keys[6], (2 * LAYERS + 1, D), 0.5, 2.0, (), jnp.float32)
    w_qkv = draw_w_qkv(jax.random.fold_in(arg_keys[12], 71), 0)
    w_out = centred(arg_keys[8], (LAYERS, D, D), D ** -0.5, 0.21875, ((1, 2),))
    w_up = centred(arg_keys[9], (LAYERS, D, MLP), D ** -0.5, 0.21875, ((2, 2),))
    w_down = centred(arg_keys[10], (LAYERS, MLP, D), MLP ** -0.5, 0.109375, ((1, 2),))
    w_decode = centred(arg_keys[11], (D, PV), D ** -0.5, 0.21875, ((1, 2),))
    return dict(traces=traces, trace_mask=trace_mask, embed_voxel=embed_voxel, embed_mask=embed_mask, position=position, norm_gain=norm_gain, norm_bias=norm_bias, w_qkv=w_qkv, w_out=w_out, w_up=w_up, w_down=w_down, w_decode=w_decode)


EPSILON = 1e-06

def layer_norm(values, gain, bias):
    average = lax.optimization_barrier(jnp.mean(values, axis=-1, keepdims=True))
    centered = values - average
    variance = lax.optimization_barrier(jnp.mean(centered * centered, axis=-1, keepdims=True))
    return centered * lax.rsqrt(variance + EPSILON) * gain + bias

def group_sum(left, right, groups):
    width = left.shape[1] // groups
    total = jnp.zeros((left.shape[0], right.shape[1]), jnp.float32)
    for group in range(groups):
        term = jnp.dot(left[:, group * width:(group + 1) * width], right[group * width:(group + 1) * width], preferred_element_type=jnp.float32)
        rounded = lax.optimization_barrier(term.astype(jnp.bfloat16))
        total = total + rounded.astype(jnp.float32)
    return total

def predict(window, live, embed_voxel, embed_mask, position, norm_gain, norm_bias, w_qkv, w_out, w_up, w_down, w_decode):
    side = WIN // PATCH
    tokens = side ** 3
    masked = window * live.astype(jnp.bfloat16)[:, :, None]
    voxels = masked.reshape(side, PATCH, side, PATCH, side, PATCH).transpose(0, 2, 4, 1, 3, 5).reshape(tokens, PATCH ** 3)
    mask_patches = live.astype(jnp.bfloat16).reshape(side, PATCH, side, PATCH).transpose(0, 2, 1, 3).reshape(side * side, PATCH * PATCH)
    stream = jnp.dot(voxels, embed_voxel, preferred_element_type=jnp.float32)
    mask_terms = jnp.dot(mask_patches, embed_mask, preferred_element_type=jnp.float32)
    stream = stream + jnp.broadcast_to(mask_terms[:, None, :], (side * side, side, D)).reshape(tokens, D)
    stream = stream + position.astype(jnp.float32)
    for layer_index in range(LAYERS):
        normed = layer_norm(stream, norm_gain[2 * layer_index], norm_bias[2 * layer_index]).astype(jnp.bfloat16)
        projected = jnp.einsum('td,sde->ste', normed.astype(jnp.float32), w_qkv[layer_index].astype(jnp.float32)).astype(jnp.bfloat16)
        query = projected[0].reshape(tokens, HEADS, HEAD_DIM).astype(jnp.float32)
        keys = projected[1].reshape(tokens, HEADS, HEAD_DIM).astype(jnp.float32)
        values = projected[2].reshape(tokens, HEADS, HEAD_DIM).astype(jnp.float32)
        scores = jnp.einsum('thd,shd->hts', query, keys) * HEAD_DIM ** (-0.5)
        weights = jax.nn.softmax(scores, axis=-1).astype(jnp.bfloat16)
        attended = jnp.einsum('hts,shd->thd', weights.astype(jnp.float32), values).astype(jnp.bfloat16).reshape(tokens, D)
        stream = stream + group_sum(attended, w_out[layer_index], N_HEAD)
        normed = layer_norm(stream, norm_gain[2 * layer_index + 1], norm_bias[2 * layer_index + 1]).astype(jnp.bfloat16)
        hidden = jax.nn.gelu(jnp.dot(normed, w_up[layer_index], preferred_element_type=jnp.float32), approximate=True).astype(jnp.bfloat16)
        stream = stream + group_sum(hidden, w_down[layer_index], N_HEAD)
    latent = layer_norm(stream, norm_gain[2 * LAYERS], norm_bias[2 * LAYERS]).astype(jnp.bfloat16)
    decoded = jnp.dot(latent, w_decode, preferred_element_type=jnp.float32).astype(jnp.bfloat16)
    return decoded.reshape(side, side, side, PATCH, PATCH, PATCH).transpose(0, 3, 1, 4, 2, 5).reshape(WIN, WIN, WIN)

def reference(traces, trace_mask, embed_voxel, embed_mask, position, norm_gain, norm_bias, w_qkv, w_out, w_up, w_down, w_decode):
    padded = jnp.concatenate([traces, jnp.zeros((HALF, WIN, WIN), traces.dtype)], 0)
    live_padded = jnp.concatenate([trace_mask, jnp.zeros((HALF, WIN), jnp.int32)], 0)

    def one_window(index):
        start = (index * HALF).astype(jnp.int32)
        window = lax.dynamic_slice_in_dim(padded, start, WIN, 0)
        live = lax.dynamic_slice_in_dim(live_padded, start, WIN, 0)
        return predict(window, live, embed_voxel, embed_mask, position, norm_gain, norm_bias, w_qkv, w_out, w_up, w_down, w_decode)
    predictions = lax.map(one_window, jnp.arange(N_TILE, dtype=jnp.int32))
    places = jnp.arange(WIN, dtype=jnp.float32)
    profile = jnp.exp(-0.5 * ((places - (WIN - 1) / 2) / (WIN / 4)) ** 2)
    lower = predictions[:, :HALF].astype(jnp.float32) * profile[:HALF, None, None]
    upper = predictions[:, HALF:].astype(jnp.float32) * profile[HALF:, None, None]
    arriving = jnp.concatenate([jnp.zeros((1, HALF, WIN, WIN), jnp.float32), upper[:-1]], 0)
    numerator = lower + arriving
    later = (jnp.arange(N_TILE, dtype=jnp.int32) > 0).astype(jnp.float32)
    denominator = profile[None, :HALF] + later[:, None] * profile[None, HALF:]
    blended = numerator / denominator[:, :, None, None]
    return blended.reshape(NIL, WIN, WIN).astype(jnp.bfloat16)
```

```python
import jax
import jax.numpy as jnp
from jax import lax
from jax.sharding import PartitionSpec as P

PATCH = 16
LAYERS = 1
WIN = 128
HEAD_DIM = 64
HALF = 64


EPSILON = 1e-06


def from_behind(block, axis, distance):
    devices = range(lax.axis_size(axis))
    route = [(i - distance, i) for i in devices if i - distance in devices]
    return lax.ppermute(block, axis, route)


def partner_sum(term):
    rounded = term.astype(jnp.bfloat16)
    other = lax.ppermute(rounded, "head", [(0, 1), (1, 0)])
    return rounded.astype(jnp.float32) + other.astype(jnp.float32)


def layer_norm(values, gain, bias):
    average = jnp.mean(values, axis=-1, keepdims=True)
    centered = values - average
    variance = jnp.mean(centered * centered, axis=-1, keepdims=True)
    return centered * lax.rsqrt(variance + EPSILON) * gain + bias


def profile_of(places):
    return jnp.exp(-0.5 * ((places - (WIN - 1) / 2) / (WIN / 4)) ** 2)


def embed_planes(amplitudes, live, embed_by_depth, embed_mask):
    side = WIN // PATCH
    depth_side = amplitudes.shape[0] // PATCH
    rows = depth_side * side * side
    masked = amplitudes * live[:, :, None]
    grouped = masked.reshape(depth_side, PATCH, side, PATCH, WIN).transpose(0, 2, 1, 3, 4)
    grouped = grouped.reshape(depth_side * side, PATCH * PATCH, WIN)
    voxels = jnp.swapaxes(grouped, 1, 2).reshape(rows, PATCH, PATCH * PATCH)
    embedded = lax.dot_general(
        voxels, embed_by_depth, (((1, 2), (0, 1)), ((), ())),
        preferred_element_type=jnp.float32,
    )
    mask_patches = (
        live.reshape(depth_side, PATCH, side, PATCH)
        .transpose(0, 2, 1, 3)
        .reshape(depth_side * side, PATCH * PATCH)
    )
    mask_terms = jnp.dot(mask_patches, embed_mask, preferred_element_type=jnp.float32)
    local_width = mask_terms.shape[1]
    return embedded + jnp.broadcast_to(
        mask_terms[:, None, :], (depth_side * side, side, local_width)
    ).reshape(rows, local_width)


def body(
    traces,
    trace_mask,
    embed_voxel,
    embed_mask,
    position,
    norm_gain,
    norm_bias,
    w_qkv,
    w_out,
    w_up,
    w_down,
    w_decode,
):
    side = WIN // PATCH
    tokens = side**3
    half_tokens = tokens // 2
    tile_index = lax.axis_index("tile")
    head_index = lax.axis_index("head")
    own_live = trace_mask.astype(jnp.bfloat16)
    next_traces, next_live = from_behind((traces, own_live), "tile", -1)
    local_width = embed_voxel.shape[1]
    embed_by_depth = embed_voxel.reshape(PATCH * PATCH, PATCH, local_width).transpose(1, 0, 2)
    own_embedded = embed_planes(traces, own_live, embed_by_depth, embed_mask)
    arrived_rows = embed_planes(next_traces, next_live, embed_by_depth, embed_mask)
    embedded = jnp.concatenate([own_embedded, arrived_rows], 0)
    embedded = (embedded + position.astype(jnp.float32)).astype(jnp.bfloat16)
    other_columns = lax.ppermute(embedded, "head", [(0, 1), (1, 0)])
    stream = jnp.where(
        head_index == 0,
        jnp.concatenate([embedded, other_columns], 1),
        jnp.concatenate([other_columns, embedded], 1),
    ).astype(jnp.float32)
    local_heads = w_qkv.shape[3] // HEAD_DIM
    normed = layer_norm(stream, norm_gain[0], norm_bias[0]).astype(jnp.bfloat16)
    projected = jnp.einsum(
        "td,sde->ste", normed, w_qkv[0], preferred_element_type=jnp.float32
    ).astype(jnp.bfloat16)
    query = projected[0].reshape(tokens, local_heads, HEAD_DIM)
    keys = projected[1].reshape(tokens, local_heads, HEAD_DIM)
    values = projected[2].reshape(tokens, local_heads, HEAD_DIM)
    scores = jnp.einsum(
        "thd,shd->hts", query, keys, preferred_element_type=jnp.float32
    ) * HEAD_DIM ** (-0.5)
    weights = jax.nn.softmax(scores, axis=-1).astype(jnp.bfloat16)
    attended = jnp.einsum(
        "hts,shd->thd", weights, values, preferred_element_type=jnp.float32
    ).astype(jnp.bfloat16)
    attended = attended.reshape(tokens, local_heads * HEAD_DIM)
    partial_attention = jnp.dot(attended, w_out[0], preferred_element_type=jnp.float32)
    stream = stream + partner_sum(partial_attention)
    normed = layer_norm(stream, norm_gain[1], norm_bias[1]).astype(jnp.bfloat16)
    hidden = jax.nn.gelu(
        jnp.dot(normed, w_up[0], preferred_element_type=jnp.float32), approximate=True
    ).astype(jnp.bfloat16)
    partial_forward = jnp.dot(hidden, w_down[0], preferred_element_type=jnp.float32)
    stream = stream + partner_sum(partial_forward)
    latent = layer_norm(stream, norm_gain[2 * LAYERS], norm_bias[2 * LAYERS]).astype(jnp.bfloat16)
    inner_rows = w_decode.shape[1] // (PATCH * PATCH)
    cell_cols = inner_rows * PATCH
    decode_by_depth = (
        w_decode.T.reshape(inner_rows, PATCH, PATCH, -1)
        .transpose(2, 0, 1, 3)
        .reshape(PATCH, cell_cols, -1)
    )
    decoded = lax.dot_general(
        latent, decode_by_depth, (((1,), (2,)), ((), ())),
        preferred_element_type=jnp.float32,
    ).astype(jnp.bfloat16)
    upper_part = from_behind(decoded[half_tokens:], "tile", 1)
    lower_part = decoded[:half_tokens]
    shape = lower_part.shape
    token_a = lax.broadcasted_iota(jnp.int32, shape, 0) // (side * side)
    inner = lax.broadcasted_iota(jnp.int32, shape, 2) // PATCH
    places = (token_a * PATCH + head_index * inner_rows + inner).astype(jnp.float32)
    lower_profile = profile_of(places)
    upper_profile = profile_of(places + HALF)
    later = (tile_index > 0).astype(jnp.float32)
    numerator = (
        lower_part.astype(jnp.float32) * lower_profile
        + upper_part.astype(jnp.float32) * upper_profile
    )
    denominator = lower_profile + later * upper_profile
    blended = (numerator / denominator).astype(jnp.bfloat16)
    half_side = side // 2
    arranged = blended.reshape(half_side * side, WIN, cell_cols)
    arranged = jnp.swapaxes(arranged, 1, 2).reshape(half_side, side, inner_rows, PATCH, WIN)
    arranged = arranged.transpose(0, 2, 1, 3, 4)
    other_rows = lax.ppermute(arranged, "head", [(0, 1), (1, 0)])
    whole = jnp.where(
        head_index == 0,
        jnp.concatenate([arranged, other_rows], 1),
        jnp.concatenate([other_rows, arranged], 1),
    )
    return whole.reshape(HALF, WIN, WIN)


def solution(mesh):
    return jax.shard_map(
        body,
        mesh=mesh,
        in_specs=(
            P("tile", None, None),
            P("tile", None),
            P(None, "head"),
            P(None, "head"),
            P(None, "head"),
            P(),
            P(),
            P(None, None, None, "head"),
            P(None, "head", None),
            P(None, None, "head"),
            P(None, "head", None),
            P(None, "head"),
        ),
        out_specs=P("tile", None, None),
        check_vma=False,
    )
```

```python
import jax
import jax.numpy as jnp
from jax import lax
from jax.sharding import PartitionSpec as P

PATCH = 16
LAYERS = 1
WIN = 128
HEAD_DIM = 64
HALF = 64


EPSILON = 1e-06


def from_behind(block, axis, distance):
    devices = range(lax.axis_size(axis))
    route = [(i - distance, i) for i in devices if i - distance in devices]
    return lax.ppermute(block, axis, route)


def partner_sum(term):
    rounded = term.astype(jnp.bfloat16)
    other = lax.ppermute(rounded, "head", [(0, 1), (1, 0)])
    return rounded.astype(jnp.float32) + other.astype(jnp.float32)


def layer_norm(values, gain, bias):
    average = jnp.mean(values, axis=-1, keepdims=True)
    centered = values - average
    variance = jnp.mean(centered * centered, axis=-1, keepdims=True)
    return centered * lax.rsqrt(variance + EPSILON) * gain + bias


def profile_of(places):
    return jnp.exp(-0.5 * ((places - (WIN - 1) / 2) / (WIN / 4)) ** 2)


def embed_planes(amplitudes, live, embed_by_depth, embed_mask):
    side = WIN // PATCH
    depth_side = amplitudes.shape[0] // PATCH
    rows = depth_side * side * side
    masked = amplitudes * live[:, :, None]
    grouped = masked.reshape(depth_side, PATCH, side, PATCH, WIN).transpose(0, 2, 1, 3, 4)
    grouped = grouped.reshape(depth_side * side, PATCH * PATCH, WIN)
    voxels = jnp.swapaxes(grouped, 1, 2).reshape(rows, PATCH, PATCH * PATCH)
    embedded = lax.dot_general(
        voxels, embed_by_depth, (((1, 2), (0, 1)), ((), ())),
        preferred_element_type=jnp.float32,
    )
    mask_patches = (
        live.reshape(depth_side, PATCH, side, PATCH)
        .transpose(0, 2, 1, 3)
        .reshape(depth_side * side, PATCH * PATCH)
    )
    mask_terms = jnp.dot(mask_patches, embed_mask, preferred_element_type=jnp.float32)
    local_width = mask_terms.shape[1]
    return embedded + jnp.broadcast_to(
        mask_terms[:, None, :], (depth_side * side, side, local_width)
    ).reshape(rows, local_width)


def body(
    traces,
    trace_mask,
    embed_voxel,
    embed_mask,
    position,
    norm_gain,
    norm_bias,
    w_qkv,
    w_out,
    w_up,
    w_down,
    w_decode,
):
    side = WIN // PATCH
    tokens = side**3
    half_tokens = tokens // 2
    tile_index = lax.axis_index("tile")
    head_index = lax.axis_index("head")
    own_live = trace_mask.astype(jnp.bfloat16)
    next_traces, next_live = from_behind((traces, own_live), "tile", -1)
    local_width = embed_voxel.shape[1]
    embed_by_depth = embed_voxel.reshape(PATCH * PATCH, PATCH, local_width).transpose(1, 0, 2)
    position = position.astype(jnp.float32)
    halves = []
    for rows, (amplitudes, live) in enumerate(((traces, own_live), (next_traces, next_live))):
        embedded = embed_planes(amplitudes, live, embed_by_depth, embed_mask)
        embedded = embedded + position[rows * half_tokens:(rows + 1) * half_tokens]
        embedded = embedded.astype(jnp.bfloat16)
        other_columns = lax.ppermute(embedded, "head", [(0, 1), (1, 0)])
        halves.append(jnp.where(
            head_index == 0,
            jnp.concatenate([embedded, other_columns], 1),
            jnp.concatenate([other_columns, embedded], 1),
        ).astype(jnp.float32))
    stream = jnp.concatenate(halves, 0)
    local_heads = w_qkv.shape[3] // HEAD_DIM
    normed = layer_norm(stream, norm_gain[0], norm_bias[0]).astype(jnp.bfloat16)
    projected = jnp.einsum(
        "td,sde->ste", normed, w_qkv[0], preferred_element_type=jnp.float32
    ).astype(jnp.bfloat16)
    keys = projected[1].reshape(tokens, local_heads, HEAD_DIM)
    values = projected[2].reshape(tokens, local_heads, HEAD_DIM)
    inner_rows = w_decode.shape[1] // (PATCH * PATCH)
    cell_cols = inner_rows * PATCH
    decode_by_depth = (
        w_decode.T.reshape(inner_rows, PATCH, PATCH, -1)
        .transpose(2, 0, 1, 3)
        .reshape(PATCH, cell_cols, -1)
    )
    decoded_chunks = {}
    for chunk in (1, 0):
        span = slice(chunk * half_tokens, (chunk + 1) * half_tokens)
        query = projected[0][span].reshape(half_tokens, local_heads, HEAD_DIM)
        scores = jnp.einsum(
            "thd,shd->hts", query, keys, preferred_element_type=jnp.float32
        ) * HEAD_DIM ** (-0.5)
        weights = jax.nn.softmax(scores, axis=-1).astype(jnp.bfloat16)
        attended = jnp.einsum(
            "hts,shd->thd", weights, values, preferred_element_type=jnp.float32
        ).astype(jnp.bfloat16)
        attended = attended.reshape(half_tokens, local_heads * HEAD_DIM)
        partial_attention = jnp.dot(attended, w_out[0], preferred_element_type=jnp.float32)
        part = stream[span] + partner_sum(partial_attention)
        normed = layer_norm(part, norm_gain[1], norm_bias[1]).astype(jnp.bfloat16)
        hidden = jax.nn.gelu(
            jnp.dot(normed, w_up[0], preferred_element_type=jnp.float32), approximate=True
        ).astype(jnp.bfloat16)
        partial_forward = jnp.dot(hidden, w_down[0], preferred_element_type=jnp.float32)
        part = part + partner_sum(partial_forward)
        latent = layer_norm(part, norm_gain[2 * LAYERS], norm_bias[2 * LAYERS]).astype(jnp.bfloat16)
        decoded_chunks[chunk] = lax.dot_general(
            latent, decode_by_depth, (((1,), (2,)), ((), ())),
            preferred_element_type=jnp.float32,
        ).astype(jnp.bfloat16)
    upper_part = from_behind(decoded_chunks[1], "tile", 1)
    lower_part = decoded_chunks[0]
    shape = lower_part.shape
    token_a = lax.broadcasted_iota(jnp.int32, shape, 0) // (side * side)
    inner = lax.broadcasted_iota(jnp.int32, shape, 2) // PATCH
    places = (token_a * PATCH + head_index * inner_rows + inner).astype(jnp.float32)
    lower_profile = profile_of(places)
    upper_profile = profile_of(places + HALF)
    later = (tile_index > 0).astype(jnp.float32)
    numerator = (
        lower_part.astype(jnp.float32) * lower_profile
        + upper_part.astype(jnp.float32) * upper_profile
    )
    denominator = lower_profile + later * upper_profile
    blended = (numerator / denominator).astype(jnp.bfloat16)
    half_side = side // 2
    arranged = blended.reshape(half_side * side, WIN, cell_cols)
    arranged = jnp.swapaxes(arranged, 1, 2).reshape(half_side, side, inner_rows, PATCH, WIN)
    arranged = arranged.transpose(0, 2, 1, 3, 4)
    other_rows = lax.ppermute(arranged, "head", [(0, 1), (1, 0)])
    whole = jnp.where(
        head_index == 0,
        jnp.concatenate([arranged, other_rows], 1),
        jnp.concatenate([other_rows, arranged], 1),
    )
    return whole.reshape(HALF, WIN, WIN)


def solution(mesh):
    return jax.shard_map(
        body,
        mesh=mesh,
        in_specs=(
            P("tile", None, None),
            P("tile", None),
            P(None, "head"),
            P(None, "head"),
            P(None, "head"),
            P(),
            P(),
            P(None, None, None, "head"),
            P(None, "head", None),
            P(None, None, "head"),
            P(None, "head", None),
            P(None, "head"),
        ),
        out_specs=P("tile", None, None),
        check_vma=False,
    )
```

```python
import jax
import jax.numpy as jnp
from jax import lax
from jax.sharding import PartitionSpec as P

PATCH = 16
LAYERS = 1
WIN = 128
HEAD_DIM = 64
HALF = 64


EPSILON = 1e-06


def from_behind(block, axis, distance):
    devices = range(lax.axis_size(axis))
    route = [(i - distance, i) for i in devices if i - distance in devices]
    return lax.ppermute(block, axis, route)


def partner_sum(term):
    rounded = term.astype(jnp.bfloat16)
    other = lax.ppermute(rounded, "head", [(0, 1), (1, 0)])
    return rounded.astype(jnp.float32) + other.astype(jnp.float32)


def layer_norm(values, gain, bias):
    average = jnp.mean(values, axis=-1, keepdims=True)
    centered = values - average
    variance = jnp.mean(centered * centered, axis=-1, keepdims=True)
    return centered * lax.rsqrt(variance + EPSILON) * gain + bias


def profile_of(places):
    return jnp.exp(-0.5 * ((places - (WIN - 1) / 2) / (WIN / 4)) ** 2)


def embed_planes(amplitudes, live, embed_by_depth, embed_mask):
    side = WIN // PATCH
    depth_side = amplitudes.shape[0] // PATCH
    rows = depth_side * side * side
    masked = amplitudes * live[:, :, None]
    grouped = masked.reshape(depth_side, PATCH, side, PATCH, WIN).transpose(0, 2, 1, 3, 4)
    grouped = grouped.reshape(depth_side * side, PATCH * PATCH, WIN)
    voxels = jnp.swapaxes(grouped, 1, 2).reshape(rows, PATCH, PATCH * PATCH)
    embedded = lax.dot_general(
        voxels, embed_by_depth, (((1, 2), (0, 1)), ((), ())),
        preferred_element_type=jnp.float32,
    )
    mask_patches = (
        live.reshape(depth_side, PATCH, side, PATCH)
        .transpose(0, 2, 1, 3)
        .reshape(depth_side * side, PATCH * PATCH)
    )
    mask_terms = jnp.dot(mask_patches, embed_mask, preferred_element_type=jnp.float32)
    local_width = mask_terms.shape[1]
    return embedded + jnp.broadcast_to(
        mask_terms[:, None, :], (depth_side * side, side, local_width)
    ).reshape(rows, local_width)


def body(
    traces,
    trace_mask,
    embed_voxel,
    embed_mask,
    position,
    norm_gain,
    norm_bias,
    w_qkv,
    w_out,
    w_up,
    w_down,
    w_decode,
):
    side = WIN // PATCH
    tokens = side**3
    half_tokens = tokens // 2
    tile_index = lax.axis_index("tile")
    head_index = lax.axis_index("head")
    own_live = trace_mask.astype(jnp.bfloat16)
    next_traces, next_live = from_behind((traces, own_live), "tile", -1)
    local_width = embed_voxel.shape[1]
    embed_by_depth = embed_voxel.reshape(PATCH * PATCH, PATCH, local_width).transpose(1, 0, 2)
    position = position.astype(jnp.float32)
    halves = []
    for rows, (amplitudes, live) in enumerate(((traces, own_live), (next_traces, next_live))):
        embedded = embed_planes(amplitudes, live, embed_by_depth, embed_mask)
        embedded = embedded + position[rows * half_tokens:(rows + 1) * half_tokens]
        embedded = embedded.astype(jnp.bfloat16)
        other_columns = lax.ppermute(embedded, "head", [(0, 1), (1, 0)])
        halves.append(jnp.where(
            head_index == 0,
            jnp.concatenate([embedded, other_columns], 1),
            jnp.concatenate([other_columns, embedded], 1),
        ).astype(jnp.float32))
    stream = jnp.concatenate(halves, 0)
    local_heads = w_qkv.shape[3] // HEAD_DIM
    normed = layer_norm(stream, norm_gain[0], norm_bias[0]).astype(jnp.bfloat16)
    projected = jnp.einsum(
        "td,sde->ste", normed, w_qkv[0], preferred_element_type=jnp.float32
    ).astype(jnp.bfloat16)
    keys = projected[1].reshape(tokens, local_heads, HEAD_DIM)
    values = projected[2].reshape(tokens, local_heads, HEAD_DIM)
    inner_rows = w_decode.shape[1] // (PATCH * PATCH)
    cell_cols = inner_rows * PATCH
    decode_by_depth = (
        w_decode.T.reshape(inner_rows, PATCH, PATCH, -1)
        .transpose(2, 0, 1, 3)
        .reshape(PATCH, cell_cols, -1)
    )
    chunks = 4
    chunk_tokens = tokens // chunks
    half_chunks = chunks // 2
    chunk_planes = (side // 2) // half_chunks
    later = (tile_index > 0).astype(jnp.float32)
    pieces = {}
    order = list(range(half_chunks, chunks)) + list(range(half_chunks))
    arrived_upper = {}
    for chunk in order:
        span = slice(chunk * chunk_tokens, (chunk + 1) * chunk_tokens)
        query = projected[0][span].reshape(chunk_tokens, local_heads, HEAD_DIM)
        scores = jnp.einsum(
            "thd,shd->hts", query, keys, preferred_element_type=jnp.float32
        ) * HEAD_DIM ** (-0.5)
        weights = jax.nn.softmax(scores, axis=-1).astype(jnp.bfloat16)
        attended = jnp.einsum(
            "hts,shd->thd", weights, values, preferred_element_type=jnp.float32
        ).astype(jnp.bfloat16)
        attended = attended.reshape(chunk_tokens, local_heads * HEAD_DIM)
        partial_attention = jnp.dot(attended, w_out[0], preferred_element_type=jnp.float32)
        part = stream[span] + partner_sum(partial_attention)
        normed = layer_norm(part, norm_gain[1], norm_bias[1]).astype(jnp.bfloat16)
        hidden = jax.nn.gelu(
            jnp.dot(normed, w_up[0], preferred_element_type=jnp.float32), approximate=True
        ).astype(jnp.bfloat16)
        partial_forward = jnp.dot(hidden, w_down[0], preferred_element_type=jnp.float32)
        part = part + partner_sum(partial_forward)
        latent = layer_norm(part, norm_gain[2 * LAYERS], norm_bias[2 * LAYERS]).astype(jnp.bfloat16)
        decoded = lax.dot_general(
            latent, decode_by_depth, (((1,), (2,)), ((), ())),
            preferred_element_type=jnp.float32,
        ).astype(jnp.bfloat16)
        if chunk >= half_chunks:
            arrived_upper[chunk - half_chunks] = from_behind(decoded, "tile", 1)
            continue
        upper_part = arrived_upper[chunk]
        shape = decoded.shape
        token_a = lax.broadcasted_iota(jnp.int32, shape, 0) // (side * side) + chunk * chunk_planes
        inner = lax.broadcasted_iota(jnp.int32, shape, 2) // PATCH
        places = (token_a * PATCH + head_index * inner_rows + inner).astype(jnp.float32)
        lower_profile = profile_of(places)
        upper_profile = profile_of(places + HALF)
        numerator = (
            decoded.astype(jnp.float32) * lower_profile
            + upper_part.astype(jnp.float32) * upper_profile
        )
        denominator = lower_profile + later * upper_profile
        blended = (numerator / denominator).astype(jnp.bfloat16)
        arranged = blended.reshape(chunk_planes * side, WIN, cell_cols)
        arranged = jnp.swapaxes(arranged, 1, 2).reshape(chunk_planes, side, inner_rows, PATCH, WIN)
        arranged = arranged.transpose(0, 2, 1, 3, 4)
        other_rows = lax.ppermute(arranged, "head", [(0, 1), (1, 0)])
        whole = jnp.where(
            head_index == 0,
            jnp.concatenate([arranged, other_rows], 1),
            jnp.concatenate([other_rows, arranged], 1),
        )
        pieces[chunk] = whole.reshape(chunk_planes * PATCH, WIN, WIN)
    return jnp.concatenate([pieces[c] for c in range(half_chunks)], 0)


def solution(mesh):
    return jax.shard_map(
        body,
        mesh=mesh,
        in_specs=(
            P("tile", None, None),
            P("tile", None),
            P(None, "head"),
            P(None, "head"),
            P(None, "head"),
            P(),
            P(),
            P(None, None, None, "head"),
            P(None, "head", None),
            P(None, None, "head"),
            P(None, "head", None),
            P(None, "head"),
        ),
        out_specs=P("tile", None, None),
        check_vma=False,
    )
```

```python
import jax
import jax.numpy as jnp
from jax import lax
from jax.sharding import PartitionSpec as P

PATCH = 16
LAYERS = 1
WIN = 128
HEAD_DIM = 64
HALF = 64


EPSILON = 1e-06


def from_behind(block, axis, distance):
    devices = range(lax.axis_size(axis))
    route = [(i - distance, i) for i in devices if i - distance in devices]
    return lax.ppermute(block, axis, route)


def partner_sum(term):
    rounded = term.astype(jnp.bfloat16)
    other = lax.ppermute(rounded, "head", [(0, 1), (1, 0)])
    return rounded.astype(jnp.float32) + other.astype(jnp.float32)


def layer_norm(values, gain, bias):
    average = jnp.mean(values, axis=-1, keepdims=True)
    centered = values - average
    variance = jnp.mean(centered * centered, axis=-1, keepdims=True)
    return centered * lax.rsqrt(variance + EPSILON) * gain + bias


def profile_of(places):
    return jnp.exp(-0.5 * ((places - (WIN - 1) / 2) / (WIN / 4)) ** 2)


def embed_planes(amplitudes, live, embed_by_depth, embed_mask):
    side = WIN // PATCH
    depth_side = amplitudes.shape[0] // PATCH
    rows = depth_side * side * side
    masked = amplitudes * live[:, :, None]
    grouped = masked.reshape(depth_side, PATCH, side, PATCH, WIN).transpose(0, 2, 1, 3, 4)
    grouped = grouped.reshape(depth_side * side, PATCH * PATCH, WIN)
    voxels = jnp.swapaxes(grouped, 1, 2).reshape(rows, PATCH, PATCH * PATCH)
    embedded = lax.dot_general(
        voxels, embed_by_depth, (((1, 2), (0, 1)), ((), ())),
        preferred_element_type=jnp.float32,
    )
    mask_patches = (
        live.reshape(depth_side, PATCH, side, PATCH)
        .transpose(0, 2, 1, 3)
        .reshape(depth_side * side, PATCH * PATCH)
    )
    mask_terms = jnp.dot(mask_patches, embed_mask, preferred_element_type=jnp.float32)
    local_width = mask_terms.shape[1]
    return embedded + jnp.broadcast_to(
        mask_terms[:, None, :], (depth_side * side, side, local_width)
    ).reshape(rows, local_width)


def body(
    traces,
    trace_mask,
    embed_voxel,
    embed_mask,
    position,
    norm_gain,
    norm_bias,
    w_qkv,
    w_out,
    w_up,
    w_down,
    w_decode,
):
    side = WIN // PATCH
    tokens = side**3
    half_tokens = tokens // 2
    tile_index = lax.axis_index("tile")
    head_index = lax.axis_index("head")
    own_live = trace_mask.astype(jnp.bfloat16)
    next_traces, next_live = from_behind((traces, own_live), "tile", -1)
    local_width = embed_voxel.shape[1]
    embed_by_depth = embed_voxel.reshape(PATCH * PATCH, PATCH, local_width).transpose(1, 0, 2)
    position = position.astype(jnp.float32)
    halves = []
    for rows, (amplitudes, live) in enumerate(((traces, own_live), (next_traces, next_live))):
        embedded = embed_planes(amplitudes, live, embed_by_depth, embed_mask)
        embedded = embedded + position[rows * half_tokens:(rows + 1) * half_tokens]
        embedded = embedded.astype(jnp.bfloat16)
        other_columns = lax.ppermute(embedded, "head", [(0, 1), (1, 0)])
        halves.append(jnp.where(
            head_index == 0,
            jnp.concatenate([embedded, other_columns], 1),
            jnp.concatenate([other_columns, embedded], 1),
        ).astype(jnp.float32))
    stream = jnp.concatenate(halves, 0)
    local_heads = w_qkv.shape[3] // HEAD_DIM
    normed = layer_norm(stream, norm_gain[0], norm_bias[0]).astype(jnp.bfloat16)
    projected = jnp.einsum(
        "td,sde->ste", normed, w_qkv[0], preferred_element_type=jnp.float32
    ).astype(jnp.bfloat16)
    keys = projected[1].reshape(tokens, local_heads, HEAD_DIM)
    values = projected[2].reshape(tokens, local_heads, HEAD_DIM)
    inner_rows = w_decode.shape[1] // (PATCH * PATCH)
    cell_cols = inner_rows * PATCH
    decode_by_depth = (
        w_decode.T.reshape(inner_rows, PATCH, PATCH, -1)
        .transpose(2, 0, 1, 3)
        .reshape(PATCH, cell_cols, -1)
    )
    decoded_chunks = {}
    for chunk in (1, 0):
        span = slice(chunk * half_tokens, (chunk + 1) * half_tokens)
        query = projected[0][span].reshape(half_tokens, local_heads, HEAD_DIM)
        scores = jnp.einsum(
            "thd,shd->hts", query, keys, preferred_element_type=jnp.float32
        ) * HEAD_DIM ** (-0.5)
        weights = jax.nn.softmax(scores, axis=-1).astype(jnp.bfloat16)
        attended = jnp.einsum(
            "hts,shd->thd", weights, values, preferred_element_type=jnp.float32
        ).astype(jnp.bfloat16)
        attended = attended.reshape(half_tokens, local_heads * HEAD_DIM)
        partial_attention = jnp.dot(attended, w_out[0], preferred_element_type=jnp.float32)
        part = stream[span] + partner_sum(partial_attention)
        normed = layer_norm(part, norm_gain[1], norm_bias[1]).astype(jnp.bfloat16)
        hidden = jax.nn.gelu(
            jnp.dot(normed, w_up[0], preferred_element_type=jnp.float32), approximate=True
        ).astype(jnp.bfloat16)
        partial_forward = jnp.dot(hidden, w_down[0], preferred_element_type=jnp.float32)
        if chunk == 0:
            decoded_chunks[1], partial_forward = lax.optimization_barrier(
                (decoded_chunks[1], partial_forward)
            )
        part = part + partner_sum(partial_forward)
        latent = layer_norm(part, norm_gain[2 * LAYERS], norm_bias[2 * LAYERS]).astype(jnp.bfloat16)
        decoded_chunks[chunk] = lax.dot_general(
            latent, decode_by_depth, (((1,), (2,)), ((), ())),
            preferred_element_type=jnp.float32,
        ).astype(jnp.bfloat16)
    upper_part = from_behind(decoded_chunks[1], "tile", 1)
    lower_part = decoded_chunks[0]
    shape = lower_part.shape
    token_a = lax.broadcasted_iota(jnp.int32, shape, 0) // (side * side)
    inner = lax.broadcasted_iota(jnp.int32, shape, 2) // PATCH
    places = (token_a * PATCH + head_index * inner_rows + inner).astype(jnp.float32)
    lower_profile = profile_of(places)
    upper_profile = profile_of(places + HALF)
    later = (tile_index > 0).astype(jnp.float32)
    numerator = (
        lower_part.astype(jnp.float32) * lower_profile
        + upper_part.astype(jnp.float32) * upper_profile
    )
    denominator = lower_profile + later * upper_profile
    blended = (numerator / denominator).astype(jnp.bfloat16)
    half_side = side // 2
    arranged = blended.reshape(half_side * side, WIN, cell_cols)
    arranged = jnp.swapaxes(arranged, 1, 2).reshape(half_side, side, inner_rows, PATCH, WIN)
    arranged = arranged.transpose(0, 2, 1, 3, 4)
    other_rows = lax.ppermute(arranged, "head", [(0, 1), (1, 0)])
    whole = jnp.where(
        head_index == 0,
        jnp.concatenate([arranged, other_rows], 1),
        jnp.concatenate([other_rows, arranged], 1),
    )
    return whole.reshape(HALF, WIN, WIN)


def solution(mesh):
    return jax.shard_map(
        body,
        mesh=mesh,
        in_specs=(
            P("tile", None, None),
            P("tile", None),
            P(None, "head"),
            P(None, "head"),
            P(None, "head"),
            P(),
            P(),
            P(None, None, None, "head"),
            P(None, "head", None),
            P(None, None, "head"),
            P(None, "head", None),
            P(None, "head"),
        ),
        out_specs=P("tile", None, None),
        check_vma=False,
    )
```

```python
import jax
import jax.numpy as jnp
from jax import lax
from jax.sharding import PartitionSpec as P

PATCH = 16
LAYERS = 1
WIN = 128
HEAD_DIM = 64
HALF = 64


EPSILON = 1e-06


def from_behind(block, axis, distance):
    devices = range(lax.axis_size(axis))
    route = [(i - distance, i) for i in devices if i - distance in devices]
    return lax.ppermute(block, axis, route)


def partner_sum(term):
    rounded = term.astype(jnp.bfloat16)
    other = lax.ppermute(rounded, "head", [(0, 1), (1, 0)])
    return rounded.astype(jnp.float32) + other.astype(jnp.float32)


def layer_norm(values, gain, bias):
    average = jnp.mean(values, axis=-1, keepdims=True)
    centered = values - average
    variance = jnp.mean(centered * centered, axis=-1, keepdims=True)
    return centered * lax.rsqrt(variance + EPSILON) * gain + bias


def profile_of(places):
    return jnp.exp(-0.5 * ((places - (WIN - 1) / 2) / (WIN / 4)) ** 2)


def embed_planes(amplitudes, live, embed_by_depth, embed_mask):
    side = WIN // PATCH
    depth_side = amplitudes.shape[0] // PATCH
    rows = depth_side * side * side
    masked = amplitudes * live[:, :, None]
    grouped = masked.reshape(depth_side, PATCH, side, PATCH, WIN).transpose(0, 2, 1, 3, 4)
    grouped = grouped.reshape(depth_side * side, PATCH * PATCH, WIN)
    voxels = jnp.swapaxes(grouped, 1, 2).reshape(rows, PATCH, PATCH * PATCH)
    embedded = lax.dot_general(
        voxels, embed_by_depth, (((1, 2), (0, 1)), ((), ())),
        preferred_element_type=jnp.float32,
    )
    mask_patches = (
        live.reshape(depth_side, PATCH, side, PATCH)
        .transpose(0, 2, 1, 3)
        .reshape(depth_side * side, PATCH * PATCH)
    )
    mask_terms = jnp.dot(mask_patches, embed_mask, preferred_element_type=jnp.float32)
    local_width = mask_terms.shape[1]
    return embedded + jnp.broadcast_to(
        mask_terms[:, None, :], (depth_side * side, side, local_width)
    ).reshape(rows, local_width)


def body(
    traces,
    trace_mask,
    embed_voxel,
    embed_mask,
    position,
    norm_gain,
    norm_bias,
    w_qkv,
    w_out,
    w_up,
    w_down,
    w_decode,
):
    side = WIN // PATCH
    tokens = side**3
    half_tokens = tokens // 2
    tile_index = lax.axis_index("tile")
    head_index = lax.axis_index("head")
    own_live = trace_mask.astype(jnp.bfloat16)
    next_traces, next_live = from_behind((traces, own_live), "tile", -1)
    local_width = embed_voxel.shape[1]
    embed_by_depth = embed_voxel.reshape(PATCH * PATCH, PATCH, local_width).transpose(1, 0, 2)
    position = position.astype(jnp.float32)
    halves = []
    for rows, (amplitudes, live) in enumerate(((traces, own_live), (next_traces, next_live))):
        embedded = embed_planes(amplitudes, live, embed_by_depth, embed_mask)
        embedded = embedded + position[rows * half_tokens:(rows + 1) * half_tokens]
        embedded = embedded.astype(jnp.bfloat16)
        other_columns = lax.ppermute(embedded, "head", [(0, 1), (1, 0)])
        halves.append(jnp.where(
            head_index == 0,
            jnp.concatenate([embedded, other_columns], 1),
            jnp.concatenate([other_columns, embedded], 1),
        ).astype(jnp.float32))
    stream = jnp.concatenate(halves, 0)
    local_heads = w_qkv.shape[3] // HEAD_DIM
    projected = jnp.concatenate([
        jnp.einsum(
            "td,sde->ste",
            layer_norm(half, norm_gain[0], norm_bias[0]).astype(jnp.bfloat16),
            w_qkv[0], preferred_element_type=jnp.float32,
        ).astype(jnp.bfloat16)
        for half in halves
    ], 1)
    keys = projected[1].reshape(tokens, local_heads, HEAD_DIM)
    values = projected[2].reshape(tokens, local_heads, HEAD_DIM)
    inner_rows = w_decode.shape[1] // (PATCH * PATCH)
    cell_cols = inner_rows * PATCH
    decode_by_depth = (
        w_decode.T.reshape(inner_rows, PATCH, PATCH, -1)
        .transpose(2, 0, 1, 3)
        .reshape(PATCH, cell_cols, -1)
    )
    decoded_chunks = {}
    for chunk in (1, 0):
        span = slice(chunk * half_tokens, (chunk + 1) * half_tokens)
        query = projected[0][span].reshape(half_tokens, local_heads, HEAD_DIM)
        scores = jnp.einsum(
            "thd,shd->hts", query, keys, preferred_element_type=jnp.float32
        ) * HEAD_DIM ** (-0.5)
        weights = jax.nn.softmax(scores, axis=-1).astype(jnp.bfloat16)
        attended = jnp.einsum(
            "hts,shd->thd", weights, values, preferred_element_type=jnp.float32
        ).astype(jnp.bfloat16)
        attended = attended.reshape(half_tokens, local_heads * HEAD_DIM)
        partial_attention = jnp.dot(attended, w_out[0], preferred_element_type=jnp.float32)
        part = stream[span] + partner_sum(partial_attention)
        normed = layer_norm(part, norm_gain[1], norm_bias[1]).astype(jnp.bfloat16)
        hidden = jax.nn.gelu(
            jnp.dot(normed, w_up[0], preferred_element_type=jnp.float32), approximate=True
        ).astype(jnp.bfloat16)
        partial_forward = jnp.dot(hidden, w_down[0], preferred_element_type=jnp.float32)
        if chunk == 0:
            decoded_chunks[1], partial_forward = lax.optimization_barrier(
                (decoded_chunks[1], partial_forward)
            )
        part = part + partner_sum(partial_forward)
        latent = layer_norm(part, norm_gain[2 * LAYERS], norm_bias[2 * LAYERS]).astype(jnp.bfloat16)
        decoded_chunks[chunk] = lax.dot_general(
            latent, decode_by_depth, (((1,), (2,)), ((), ())),
            preferred_element_type=jnp.float32,
        ).astype(jnp.bfloat16)
    upper_part = from_behind(decoded_chunks[1], "tile", 1)
    lower_part = decoded_chunks[0]
    later = (tile_index > 0).astype(jnp.float32)
    half_side = side // 2
    pieces = []
    piece_planes = half_side // 2
    piece_tokens = piece_planes * side * side
    for piece in range(half_side // piece_planes):
        span = slice(piece * piece_tokens, (piece + 1) * piece_tokens)
        lower_piece = lower_part[span]
        shape = lower_piece.shape
        token_a = lax.broadcasted_iota(jnp.int32, shape, 0) // (side * side) + piece * piece_planes
        inner = lax.broadcasted_iota(jnp.int32, shape, 2) // PATCH
        places = (token_a * PATCH + head_index * inner_rows + inner).astype(jnp.float32)
        lower_profile = profile_of(places)
        upper_profile = profile_of(places + HALF)
        numerator = (
            lower_piece.astype(jnp.float32) * lower_profile
            + upper_part[span].astype(jnp.float32) * upper_profile
        )
        denominator = lower_profile + later * upper_profile
        blended = (numerator / denominator).astype(jnp.bfloat16)
        arranged = blended.reshape(piece_planes * side, WIN, cell_cols)
        arranged = jnp.swapaxes(arranged, 1, 2).reshape(piece_planes, side, inner_rows, PATCH, WIN)
        other_rows = lax.ppermute(arranged, "head", [(0, 1), (1, 0)])
        whole = jnp.where(
            head_index == 0,
            jnp.concatenate([arranged, other_rows], 2),
            jnp.concatenate([other_rows, arranged], 2),
        )
        pieces.append(whole.transpose(0, 2, 1, 3, 4).reshape(piece_planes * PATCH, WIN, WIN))
    return jnp.concatenate(pieces, 0)


def solution(mesh):
    return jax.shard_map(
        body,
        mesh=mesh,
        in_specs=(
            P("tile", None, None),
            P("tile", None),
            P(None, "head"),
            P(None, "head"),
            P(None, "head"),
            P(),
            P(),
            P(None, None, None, "head"),
            P(None, "head", None),
            P(None, None, "head"),
            P(None, "head", None),
            P(None, "head"),
        ),
        out_specs=P("tile", None, None),
        check_vma=False,
    )
```

```python
import jax
import jax.numpy as jnp
from jax import lax
from jax.sharding import PartitionSpec as P

PATCH = 16
LAYERS = 1
WIN = 128
HEAD_DIM = 64
HALF = 64


EPSILON = 1e-06


def from_behind(block, axis, distance):
    devices = range(lax.axis_size(axis))
    route = [(i - distance, i) for i in devices if i - distance in devices]
    return lax.ppermute(block, axis, route)


def partner_sum(term):
    rounded = term.astype(jnp.bfloat16)
    other = lax.ppermute(rounded, "head", [(0, 1), (1, 0)])
    return rounded.astype(jnp.float32) + other.astype(jnp.float32)


def layer_norm(values, gain, bias):
    average = jnp.mean(values, axis=-1, keepdims=True)
    centered = values - average
    variance = jnp.mean(centered * centered, axis=-1, keepdims=True)
    return centered * lax.rsqrt(variance + EPSILON) * gain + bias


def profile_of(places):
    return jnp.exp(-0.5 * ((places - (WIN - 1) / 2) / (WIN / 4)) ** 2)


def embed_planes(amplitudes, live, embed_by_depth, embed_mask):
    side = WIN // PATCH
    depth_side = amplitudes.shape[0] // PATCH
    rows = depth_side * side * side
    masked = amplitudes * live[:, :, None]
    grouped = masked.reshape(depth_side, PATCH, side, PATCH, WIN).transpose(0, 2, 1, 3, 4)
    grouped = grouped.reshape(depth_side * side, PATCH * PATCH, WIN)
    voxels = jnp.swapaxes(grouped, 1, 2).reshape(rows, PATCH, PATCH * PATCH)
    embedded = lax.dot_general(
        voxels, embed_by_depth, (((1, 2), (0, 1)), ((), ())),
        preferred_element_type=jnp.float32,
    )
    mask_patches = (
        live.reshape(depth_side, PATCH, side, PATCH)
        .transpose(0, 2, 1, 3)
        .reshape(depth_side * side, PATCH * PATCH)
    )
    mask_terms = jnp.dot(mask_patches, embed_mask, preferred_element_type=jnp.float32)
    local_width = mask_terms.shape[1]
    return embedded + jnp.broadcast_to(
        mask_terms[:, None, :], (depth_side * side, side, local_width)
    ).reshape(rows, local_width)


def body(
    traces,
    trace_mask,
    embed_voxel,
    embed_mask,
    position,
    norm_gain,
    norm_bias,
    w_qkv,
    w_out,
    w_up,
    w_down,
    w_decode,
):
    side = WIN // PATCH
    tokens = side**3
    half_tokens = tokens // 2
    tile_index = lax.axis_index("tile")
    head_index = lax.axis_index("head")
    own_live = trace_mask.astype(jnp.bfloat16)
    next_traces, next_live = from_behind((traces, own_live), "tile", -1)
    other_w_out = lax.ppermute(w_out[0], "head", [(0, 1), (1, 0)])
    local_width = embed_voxel.shape[1]
    embed_by_depth = embed_voxel.reshape(PATCH * PATCH, PATCH, local_width).transpose(1, 0, 2)
    position = position.astype(jnp.float32)
    halves = []
    for rows, (amplitudes, live) in enumerate(((traces, own_live), (next_traces, next_live))):
        embedded = embed_planes(amplitudes, live, embed_by_depth, embed_mask)
        embedded = embedded + position[rows * half_tokens:(rows + 1) * half_tokens]
        embedded = embedded.astype(jnp.bfloat16)
        other_columns = lax.ppermute(embedded, "head", [(0, 1), (1, 0)])
        halves.append(jnp.where(
            head_index == 0,
            jnp.concatenate([embedded, other_columns], 1),
            jnp.concatenate([other_columns, embedded], 1),
        ).astype(jnp.float32))
    stream = jnp.concatenate(halves, 0)
    local_heads = w_qkv.shape[3] // HEAD_DIM
    normed = layer_norm(stream, norm_gain[0], norm_bias[0]).astype(jnp.bfloat16)
    projected = jnp.einsum(
        "td,sde->ste", normed, w_qkv[0], preferred_element_type=jnp.float32
    ).astype(jnp.bfloat16)
    keys = projected[1].reshape(tokens, local_heads, HEAD_DIM)
    values = projected[2].reshape(tokens, local_heads, HEAD_DIM)
    inner_rows = w_decode.shape[1] // (PATCH * PATCH)
    cell_cols = inner_rows * PATCH
    decode_by_depth = (
        w_decode.T.reshape(inner_rows, PATCH, PATCH, -1)
        .transpose(2, 0, 1, 3)
        .reshape(PATCH, cell_cols, -1)
    )
    decoded_chunks = {}
    for chunk in (1, 0):
        span = slice(chunk * half_tokens, (chunk + 1) * half_tokens)
        query = projected[0][span].reshape(half_tokens, local_heads, HEAD_DIM)
        scores = jnp.einsum(
            "thd,shd->hts", query, keys, preferred_element_type=jnp.float32
        ) * HEAD_DIM ** (-0.5)
        weights = jax.nn.softmax(scores, axis=-1).astype(jnp.bfloat16)
        attended = jnp.einsum(
            "hts,shd->thd", weights, values, preferred_element_type=jnp.float32
        ).astype(jnp.bfloat16)
        attended = attended.reshape(half_tokens, local_heads * HEAD_DIM)
        other_attended = lax.ppermute(attended, "head", [(0, 1), (1, 0)])
        own_term = jnp.dot(attended, w_out[0], preferred_element_type=jnp.float32)
        other_term = jnp.dot(other_attended, other_w_out, preferred_element_type=jnp.float32)
        part = stream[span] + (
            own_term.astype(jnp.bfloat16).astype(jnp.float32)
            + other_term.astype(jnp.bfloat16).astype(jnp.float32)
        )
        normed = layer_norm(part, norm_gain[1], norm_bias[1]).astype(jnp.bfloat16)
        hidden = jax.nn.gelu(
            jnp.dot(normed, w_up[0], preferred_element_type=jnp.float32), approximate=True
        ).astype(jnp.bfloat16)
        partial_forward = jnp.dot(hidden, w_down[0], preferred_element_type=jnp.float32)
        if chunk == 0:
            decoded_chunks[1], partial_forward = lax.optimization_barrier(
                (decoded_chunks[1], partial_forward)
            )
        part = part + partner_sum(partial_forward)
        latent = layer_norm(part, norm_gain[2 * LAYERS], norm_bias[2 * LAYERS]).astype(jnp.bfloat16)
        decoded_chunks[chunk] = lax.dot_general(
            latent, decode_by_depth, (((1,), (2,)), ((), ())),
            preferred_element_type=jnp.float32,
        ).astype(jnp.bfloat16)
    upper_part = from_behind(decoded_chunks[1], "tile", 1)
    lower_part = decoded_chunks[0]
    shape = lower_part.shape
    token_a = lax.broadcasted_iota(jnp.int32, shape, 0) // (side * side)
    inner = lax.broadcasted_iota(jnp.int32, shape, 2) // PATCH
    places = (token_a * PATCH + head_index * inner_rows + inner).astype(jnp.float32)
    lower_profile = profile_of(places)
    upper_profile = profile_of(places + HALF)
    later = (tile_index > 0).astype(jnp.float32)
    numerator = (
        lower_part.astype(jnp.float32) * lower_profile
        + upper_part.astype(jnp.float32) * upper_profile
    )
    denominator = lower_profile + later * upper_profile
    blended = (numerator / denominator).astype(jnp.bfloat16)
    half_side = side // 2
    arranged = blended.reshape(half_side * side, WIN, cell_cols)
    arranged = jnp.swapaxes(arranged, 1, 2).reshape(half_side, side, inner_rows, PATCH, WIN)
    arranged = arranged.transpose(0, 2, 1, 3, 4)
    other_rows = lax.ppermute(arranged, "head", [(0, 1), (1, 0)])
    whole = jnp.where(
        head_index == 0,
        jnp.concatenate([arranged, other_rows], 1),
        jnp.concatenate([other_rows, arranged], 1),
    )
    return whole.reshape(HALF, WIN, WIN)


def solution(mesh):
    return jax.shard_map(
        body,
        mesh=mesh,
        in_specs=(
            P("tile", None, None),
            P("tile", None),
            P(None, "head"),
            P(None, "head"),
            P(None, "head"),
            P(),
            P(),
            P(None, None, None, "head"),
            P(None, "head", None),
            P(None, None, "head"),
            P(None, "head", None),
            P(None, "head"),
        ),
        out_specs=P("tile", None, None),
        check_vma=False,
    )
```

```python
import jax
import jax.numpy as jnp
from jax import lax
from jax.sharding import PartitionSpec as P

PATCH = 16
LAYERS = 1
WIN = 128
HEAD_DIM = 64
HALF = 64


EPSILON = 1e-06


def from_behind(block, axis, distance):
    devices = range(lax.axis_size(axis))
    route = [(i - distance, i) for i in devices if i - distance in devices]
    return lax.ppermute(block, axis, route)


def partner_sum(term):
    rounded = term.astype(jnp.bfloat16)
    other = lax.ppermute(rounded, "head", [(0, 1), (1, 0)])
    return rounded.astype(jnp.float32) + other.astype(jnp.float32)


def layer_norm(values, gain, bias):
    average = jnp.mean(values, axis=-1, keepdims=True)
    centered = values - average
    variance = jnp.mean(centered * centered, axis=-1, keepdims=True)
    return centered * lax.rsqrt(variance + EPSILON) * gain + bias


def profile_of(places):
    return jnp.exp(-0.5 * ((places - (WIN - 1) / 2) / (WIN / 4)) ** 2)


def embed_planes(amplitudes, live, embed_by_depth, embed_mask):
    side = WIN // PATCH
    depth_side = amplitudes.shape[0] // PATCH
    rows = depth_side * side * side
    masked = amplitudes * live[:, :, None]
    grouped = masked.reshape(depth_side, PATCH, side, PATCH, WIN).transpose(0, 2, 1, 3, 4)
    grouped = grouped.reshape(depth_side * side, PATCH * PATCH, WIN)
    voxels = jnp.swapaxes(grouped, 1, 2).reshape(rows, PATCH, PATCH * PATCH)
    embedded = lax.dot_general(
        voxels, embed_by_depth, (((1, 2), (0, 1)), ((), ())),
        preferred_element_type=jnp.float32,
    )
    mask_patches = (
        live.reshape(depth_side, PATCH, side, PATCH)
        .transpose(0, 2, 1, 3)
        .reshape(depth_side * side, PATCH * PATCH)
    )
    mask_terms = jnp.dot(mask_patches, embed_mask, preferred_element_type=jnp.float32)
    local_width = mask_terms.shape[1]
    return embedded + jnp.broadcast_to(
        mask_terms[:, None, :], (depth_side * side, side, local_width)
    ).reshape(rows, local_width)


def body(
    traces,
    trace_mask,
    embed_voxel,
    embed_mask,
    position,
    norm_gain,
    norm_bias,
    w_qkv,
    w_out,
    w_up,
    w_down,
    w_decode,
):
    side = WIN // PATCH
    tokens = side**3
    half_tokens = tokens // 2
    tile_index = lax.axis_index("tile")
    head_index = lax.axis_index("head")
    own_live = trace_mask.astype(jnp.bfloat16)
    other_w_out = lax.ppermute(w_out[0], "head", [(0, 1), (1, 0)])
    local_width = embed_voxel.shape[1]
    embed_by_depth = embed_voxel.reshape(PATCH * PATCH, PATCH, local_width).transpose(1, 0, 2)
    position = position.astype(jnp.float32)
    own_embedded = embed_planes(traces, own_live, embed_by_depth, embed_mask)
    next_embedded = from_behind(own_embedded, "tile", -1)
    halves = []
    for rows, embedded in enumerate((own_embedded, next_embedded)):
        embedded = embedded + position[rows * half_tokens:(rows + 1) * half_tokens]
        embedded = embedded.astype(jnp.bfloat16)
        other_columns = lax.ppermute(embedded, "head", [(0, 1), (1, 0)])
        halves.append(jnp.where(
            head_index == 0,
            jnp.concatenate([embedded, other_columns], 1),
            jnp.concatenate([other_columns, embedded], 1),
        ).astype(jnp.float32))
    stream = jnp.concatenate(halves, 0)
    local_heads = w_qkv.shape[3] // HEAD_DIM
    normed = layer_norm(stream, norm_gain[0], norm_bias[0]).astype(jnp.bfloat16)
    projected = jnp.einsum(
        "td,sde->ste", normed, w_qkv[0], preferred_element_type=jnp.float32
    ).astype(jnp.bfloat16)
    keys = projected[1].reshape(tokens, local_heads, HEAD_DIM)
    values = projected[2].reshape(tokens, local_heads, HEAD_DIM)
    inner_rows = w_decode.shape[1] // (PATCH * PATCH)
    cell_cols = inner_rows * PATCH
    decode_by_depth = (
        w_decode.T.reshape(inner_rows, PATCH, PATCH, -1)
        .transpose(2, 0, 1, 3)
        .reshape(PATCH, cell_cols, -1)
    )
    decoded_chunks = {}
    for chunk in (1, 0):
        span = slice(chunk * half_tokens, (chunk + 1) * half_tokens)
        query = projected[0][span].reshape(half_tokens, local_heads, HEAD_DIM)
        scores = jnp.einsum(
            "thd,shd->hts", query, keys, preferred_element_type=jnp.float32
        ) * HEAD_DIM ** (-0.5)
        weights = jax.nn.softmax(scores, axis=-1).astype(jnp.bfloat16)
        attended = jnp.einsum(
            "hts,shd->thd", weights, values, preferred_element_type=jnp.float32
        ).astype(jnp.bfloat16)
        attended = attended.reshape(half_tokens, local_heads * HEAD_DIM)
        other_attended = lax.ppermute(attended, "head", [(0, 1), (1, 0)])
        own_term = jnp.dot(attended, w_out[0], preferred_element_type=jnp.float32)
        other_term = jnp.dot(other_attended, other_w_out, preferred_element_type=jnp.float32)
        part = stream[span] + (
            own_term.astype(jnp.bfloat16).astype(jnp.float32)
            + other_term.astype(jnp.bfloat16).astype(jnp.float32)
        )
        normed = layer_norm(part, norm_gain[1], norm_bias[1]).astype(jnp.bfloat16)
        hidden = jax.nn.gelu(
            jnp.dot(normed, w_up[0], preferred_element_type=jnp.float32), approximate=True
        ).astype(jnp.bfloat16)
        partial_forward = jnp.dot(hidden, w_down[0], preferred_element_type=jnp.float32)
        if chunk == 0:
            sent_latent, partial_forward = lax.optimization_barrier(
                (sent_latent, partial_forward)
            )
        part = part + partner_sum(partial_forward)
        latent = layer_norm(part, norm_gain[2 * LAYERS], norm_bias[2 * LAYERS]).astype(jnp.bfloat16)
        if chunk == 1:
            sent_latent = latent
            continue
        decoded_chunks[chunk] = lax.dot_general(
            latent, decode_by_depth, (((1,), (2,)), ((), ())),
            preferred_element_type=jnp.float32,
        ).astype(jnp.bfloat16)
    arrived_latent = from_behind(sent_latent, "tile", 1)
    upper_part = lax.dot_general(
        arrived_latent, decode_by_depth, (((1,), (2,)), ((), ())),
        preferred_element_type=jnp.float32,
    ).astype(jnp.bfloat16)
    lower_part = decoded_chunks[0]
    shape = lower_part.shape
    token_a = lax.broadcasted_iota(jnp.int32, shape, 0) // (side * side)
    inner = lax.broadcasted_iota(jnp.int32, shape, 2) // PATCH
    places = (token_a * PATCH + head_index * inner_rows + inner).astype(jnp.float32)
    lower_profile = profile_of(places)
    upper_profile = profile_of(places + HALF)
    later = (tile_index > 0).astype(jnp.float32)
    numerator = (
        lower_part.astype(jnp.float32) * lower_profile
        + upper_part.astype(jnp.float32) * upper_profile
    )
    denominator = lower_profile + later * upper_profile
    blended = (numerator / denominator).astype(jnp.bfloat16)
    half_side = side // 2
    arranged = blended.reshape(half_side * side, WIN, cell_cols)
    arranged = jnp.swapaxes(arranged, 1, 2).reshape(half_side, side, inner_rows, PATCH, WIN)
    arranged = arranged.transpose(0, 2, 1, 3, 4)
    other_rows = lax.ppermute(arranged, "head", [(0, 1), (1, 0)])
    whole = jnp.where(
        head_index == 0,
        jnp.concatenate([arranged, other_rows], 1),
        jnp.concatenate([other_rows, arranged], 1),
    )
    return whole.reshape(HALF, WIN, WIN)


def solution(mesh):
    return jax.shard_map(
        body,
        mesh=mesh,
        in_specs=(
            P("tile", None, None),
            P("tile", None),
            P(None, "head"),
            P(None, "head"),
            P(None, "head"),
            P(),
            P(),
            P(None, None, None, "head"),
            P(None, "head", None),
            P(None, None, "head"),
            P(None, "head", None),
            P(None, "head"),
        ),
        out_specs=P("tile", None, None),
        check_vma=False,
    )
```

```python
import jax
import jax.numpy as jnp
from jax import lax
from jax.sharding import PartitionSpec as P

PATCH = 16
LAYERS = 1
WIN = 128
HEAD_DIM = 64
HALF = 64


EPSILON = 1e-06


def from_behind(block, axis, distance):
    devices = range(lax.axis_size(axis))
    route = [(i - distance, i) for i in devices if i - distance in devices]
    return lax.ppermute(block, axis, route)


def partner_sum(term):
    rounded = term.astype(jnp.bfloat16)
    other = lax.ppermute(rounded, "head", [(0, 1), (1, 0)])
    return rounded.astype(jnp.float32) + other.astype(jnp.float32)


def layer_norm(values, gain, bias):
    average = jnp.mean(values, axis=-1, keepdims=True)
    centered = values - average
    variance = jnp.mean(centered * centered, axis=-1, keepdims=True)
    return centered * lax.rsqrt(variance + EPSILON) * gain + bias


def profile_of(places):
    return jnp.exp(-0.5 * ((places - (WIN - 1) / 2) / (WIN / 4)) ** 2)


def embed_planes(amplitudes, live, embed_by_depth, embed_mask):
    side = WIN // PATCH
    depth_side = amplitudes.shape[0] // PATCH
    rows = depth_side * side * side
    masked = amplitudes * live[:, :, None]
    grouped = masked.reshape(depth_side, PATCH, side, PATCH, WIN).transpose(0, 2, 1, 3, 4)
    grouped = grouped.reshape(depth_side * side, PATCH * PATCH, WIN)
    voxels = jnp.swapaxes(grouped, 1, 2).reshape(rows, PATCH, PATCH * PATCH)
    embedded = lax.dot_general(
        voxels, embed_by_depth, (((1, 2), (0, 1)), ((), ())),
        preferred_element_type=jnp.float32,
    )
    mask_patches = (
        live.reshape(depth_side, PATCH, side, PATCH)
        .transpose(0, 2, 1, 3)
        .reshape(depth_side * side, PATCH * PATCH)
    )
    mask_terms = jnp.dot(mask_patches, embed_mask, preferred_element_type=jnp.float32)
    local_width = mask_terms.shape[1]
    return embedded + jnp.broadcast_to(
        mask_terms[:, None, :], (depth_side * side, side, local_width)
    ).reshape(rows, local_width)


def body(
    traces,
    trace_mask,
    embed_voxel,
    embed_mask,
    position,
    norm_gain,
    norm_bias,
    w_qkv,
    w_out,
    w_up,
    w_down,
    w_decode,
):
    side = WIN // PATCH
    tokens = side**3
    half_tokens = tokens // 2
    tile_index = lax.axis_index("tile")
    head_index = lax.axis_index("head")
    own_live = trace_mask.astype(jnp.bfloat16)
    local_width = embed_voxel.shape[1]
    embed_by_depth = embed_voxel.reshape(PATCH * PATCH, PATCH, local_width).transpose(1, 0, 2)
    position = position.astype(jnp.float32)
    own_embedded = embed_planes(traces, own_live, embed_by_depth, embed_mask)
    next_embedded = from_behind(own_embedded, "tile", -1)
    halves = []
    for rows, embedded in enumerate((own_embedded, next_embedded)):
        embedded = embedded + position[rows * half_tokens:(rows + 1) * half_tokens]
        embedded = embedded.astype(jnp.bfloat16)
        other_columns = lax.ppermute(embedded, "head", [(0, 1), (1, 0)])
        halves.append(jnp.where(
            head_index == 0,
            jnp.concatenate([embedded, other_columns], 1),
            jnp.concatenate([other_columns, embedded], 1),
        ).astype(jnp.float32))
    own_w_out, halves = lax.optimization_barrier((w_out[0], halves))
    other_w_out = lax.ppermute(own_w_out, "head", [(0, 1), (1, 0)])
    stream = jnp.concatenate(halves, 0)
    local_heads = w_qkv.shape[3] // HEAD_DIM
    normed = layer_norm(stream, norm_gain[0], norm_bias[0]).astype(jnp.bfloat16)
    projected = jnp.einsum(
        "td,sde->ste", normed, w_qkv[0], preferred_element_type=jnp.float32
    ).astype(jnp.bfloat16)
    keys = projected[1].reshape(tokens, local_heads, HEAD_DIM)
    values = projected[2].reshape(tokens, local_heads, HEAD_DIM)
    inner_rows = w_decode.shape[1] // (PATCH * PATCH)
    cell_cols = inner_rows * PATCH
    decode_by_depth = (
        w_decode.T.reshape(inner_rows, PATCH, PATCH, -1)
        .transpose(2, 0, 1, 3)
        .reshape(PATCH, cell_cols, -1)
    )
    decoded_chunks = {}
    for chunk in (1, 0):
        span = slice(chunk * half_tokens, (chunk + 1) * half_tokens)
        query = projected[0][span].reshape(half_tokens, local_heads, HEAD_DIM)
        scores = jnp.einsum(
            "thd,shd->hts", query, keys, preferred_element_type=jnp.float32
        ) * HEAD_DIM ** (-0.5)
        weights = jax.nn.softmax(scores, axis=-1).astype(jnp.bfloat16)
        attended = jnp.einsum(
            "hts,shd->thd", weights, values, preferred_element_type=jnp.float32
        ).astype(jnp.bfloat16)
        attended = attended.reshape(half_tokens, local_heads * HEAD_DIM)
        other_attended = lax.ppermute(attended, "head", [(0, 1), (1, 0)])
        own_term = jnp.dot(attended, own_w_out, preferred_element_type=jnp.float32)
        other_term = jnp.dot(other_attended, other_w_out, preferred_element_type=jnp.float32)
        part = stream[span] + (
            own_term.astype(jnp.bfloat16).astype(jnp.float32)
            + other_term.astype(jnp.bfloat16).astype(jnp.float32)
        )
        normed = layer_norm(part, norm_gain[1], norm_bias[1]).astype(jnp.bfloat16)
        hidden = jax.nn.gelu(
            jnp.dot(normed, w_up[0], preferred_element_type=jnp.float32), approximate=True
        ).astype(jnp.bfloat16)
        partial_forward = jnp.dot(hidden, w_down[0], preferred_element_type=jnp.float32)
        if chunk == 0:
            sent_latent, partial_forward = lax.optimization_barrier(
                (sent_latent, partial_forward)
            )
        part = part + partner_sum(partial_forward)
        latent = layer_norm(part, norm_gain[2 * LAYERS], norm_bias[2 * LAYERS]).astype(jnp.bfloat16)
        if chunk == 1:
            sent_latent = latent
            continue
        decoded_chunks[chunk] = lax.dot_general(
            latent, decode_by_depth, (((1,), (2,)), ((), ())),
            preferred_element_type=jnp.float32,
        ).astype(jnp.bfloat16)
    arrived_latent = from_behind(sent_latent, "tile", 1)
    upper_part = lax.dot_general(
        arrived_latent, decode_by_depth, (((1,), (2,)), ((), ())),
        preferred_element_type=jnp.float32,
    ).astype(jnp.bfloat16)
    lower_part = decoded_chunks[0]
    shape = lower_part.shape
    token_a = lax.broadcasted_iota(jnp.int32, shape, 0) // (side * side)
    inner = lax.broadcasted_iota(jnp.int32, shape, 2) // PATCH
    places = (token_a * PATCH + head_index * inner_rows + inner).astype(jnp.float32)
    lower_profile = profile_of(places)
    upper_profile = profile_of(places + HALF)
    later = (tile_index > 0).astype(jnp.float32)
    numerator = (
        lower_part.astype(jnp.float32) * lower_profile
        + upper_part.astype(jnp.float32) * upper_profile
    )
    denominator = lower_profile + later * upper_profile
    blended = (numerator / denominator).astype(jnp.bfloat16)
    half_side = side // 2
    arranged = blended.reshape(half_side * side, WIN, cell_cols)
    arranged = jnp.swapaxes(arranged, 1, 2).reshape(half_side, side, inner_rows, PATCH, WIN)
    arranged = arranged.transpose(0, 2, 1, 3, 4)
    other_rows = lax.ppermute(arranged, "head", [(0, 1), (1, 0)])
    whole = jnp.where(
        head_index == 0,
        jnp.concatenate([arranged, other_rows], 1),
        jnp.concatenate([other_rows, arranged], 1),
    )
    return whole.reshape(HALF, WIN, WIN)


def solution(mesh):
    return jax.shard_map(
        body,
        mesh=mesh,
        in_specs=(
            P("tile", None, None),
            P("tile", None),
            P(None, "head"),
            P(None, "head"),
            P(None, "head"),
            P(),
            P(),
            P(None, None, None, "head"),
            P(None, "head", None),
            P(None, None, "head"),
            P(None, "head", None),
            P(None, "head"),
        ),
        out_specs=P("tile", None, None),
        check_vma=False,
    )
```

```python
import jax
import jax.numpy as jnp
from jax import lax
from jax.sharding import PartitionSpec as P

PATCH = 16
LAYERS = 1
WIN = 128
HEAD_DIM = 64
HALF = 64


EPSILON = 1e-06


def from_behind(block, axis, distance):
    devices = range(lax.axis_size(axis))
    route = [(i - distance, i) for i in devices if i - distance in devices]
    return lax.ppermute(block, axis, route)


def partner_sum(term):
    rounded = term.astype(jnp.bfloat16)
    other = lax.ppermute(rounded, "head", [(0, 1), (1, 0)])
    return rounded.astype(jnp.float32) + other.astype(jnp.float32)


def layer_norm(values, gain, bias):
    average = jnp.mean(values, axis=-1, keepdims=True)
    centered = values - average
    variance = jnp.mean(centered * centered, axis=-1, keepdims=True)
    return centered * lax.rsqrt(variance + EPSILON) * gain + bias


def profile_of(places):
    return jnp.exp(-0.5 * ((places - (WIN - 1) / 2) / (WIN / 4)) ** 2)


def embed_planes(amplitudes, live, embed_by_depth, embed_mask):
    side = WIN // PATCH
    depth_side = amplitudes.shape[0] // PATCH
    rows = depth_side * side * side
    masked = amplitudes * live[:, :, None]
    grouped = masked.reshape(depth_side, PATCH, side, PATCH, WIN).transpose(0, 2, 1, 3, 4)
    grouped = grouped.reshape(depth_side * side, PATCH * PATCH, WIN)
    voxels = jnp.swapaxes(grouped, 1, 2).reshape(rows, PATCH, PATCH * PATCH)
    embedded = lax.dot_general(
        voxels, embed_by_depth, (((1, 2), (0, 1)), ((), ())),
        preferred_element_type=jnp.float32,
    )
    mask_patches = (
        live.reshape(depth_side, PATCH, side, PATCH)
        .transpose(0, 2, 1, 3)
        .reshape(depth_side * side, PATCH * PATCH)
    )
    mask_terms = jnp.dot(mask_patches, embed_mask, preferred_element_type=jnp.float32)
    local_width = mask_terms.shape[1]
    return embedded + jnp.broadcast_to(
        mask_terms[:, None, :], (depth_side * side, side, local_width)
    ).reshape(rows, local_width)


def body(
    traces,
    trace_mask,
    embed_voxel,
    embed_mask,
    position,
    norm_gain,
    norm_bias,
    w_qkv,
    w_out,
    w_up,
    w_down,
    w_decode,
):
    side = WIN // PATCH
    tokens = side**3
    half_tokens = tokens // 2
    tile_index = lax.axis_index("tile")
    head_index = lax.axis_index("head")
    own_live = trace_mask.astype(jnp.bfloat16)
    other_w_out = lax.ppermute(w_out[0], "head", [(0, 1), (1, 0)])
    local_width = embed_voxel.shape[1]
    embed_by_depth = embed_voxel.reshape(PATCH * PATCH, PATCH, local_width).transpose(1, 0, 2)
    position = position.astype(jnp.float32)
    own_embedded = embed_planes(traces, own_live, embed_by_depth, embed_mask)
    next_embedded = from_behind(own_embedded, "tile", -1)
    halves = []
    for rows, embedded in enumerate((own_embedded, next_embedded)):
        embedded = embedded + position[rows * half_tokens:(rows + 1) * half_tokens]
        embedded = embedded.astype(jnp.bfloat16)
        other_columns = lax.ppermute(embedded, "head", [(0, 1), (1, 0)])
        halves.append(jnp.where(
            head_index == 0,
            jnp.concatenate([embedded, other_columns], 1),
            jnp.concatenate([other_columns, embedded], 1),
        ).astype(jnp.float32))
    stream = jnp.concatenate(halves, 0)
    local_heads = w_qkv.shape[3] // HEAD_DIM
    normed = layer_norm(stream, norm_gain[0], norm_bias[0]).astype(jnp.bfloat16)
    projected = jnp.einsum(
        "td,sde->ste", normed, w_qkv[0], preferred_element_type=jnp.float32
    ).astype(jnp.bfloat16)
    keys = projected[1].reshape(tokens, local_heads, HEAD_DIM)
    values = projected[2].reshape(tokens, local_heads, HEAD_DIM)
    inner_rows = w_decode.shape[1] // (PATCH * PATCH)
    cell_cols = inner_rows * PATCH
    decode_by_depth = (
        w_decode.T.reshape(inner_rows, PATCH, PATCH, -1)
        .transpose(2, 0, 1, 3)
        .reshape(PATCH, cell_cols, -1)
    )
    for chunk in (1, 0):
        span = slice(chunk * half_tokens, (chunk + 1) * half_tokens)
        query = projected[0][span].reshape(half_tokens, local_heads, HEAD_DIM)
        scores = jnp.einsum(
            "thd,shd->hts", query, keys, preferred_element_type=jnp.float32
        ) * HEAD_DIM ** (-0.5)
        weights = jax.nn.softmax(scores, axis=-1).astype(jnp.bfloat16)
        attended = jnp.einsum(
            "hts,shd->thd", weights, values, preferred_element_type=jnp.float32
        ).astype(jnp.bfloat16)
        attended = attended.reshape(half_tokens, local_heads * HEAD_DIM)
        other_attended = lax.ppermute(attended, "head", [(0, 1), (1, 0)])
        own_term = jnp.dot(attended, w_out[0], preferred_element_type=jnp.float32)
        other_term = jnp.dot(other_attended, other_w_out, preferred_element_type=jnp.float32)
        part = stream[span] + (
            own_term.astype(jnp.bfloat16).astype(jnp.float32)
            + other_term.astype(jnp.bfloat16).astype(jnp.float32)
        )
        normed = layer_norm(part, norm_gain[1], norm_bias[1]).astype(jnp.bfloat16)
        hidden = jax.nn.gelu(
            jnp.dot(normed, w_up[0], preferred_element_type=jnp.float32), approximate=True
        ).astype(jnp.bfloat16)
        partial_forward = jnp.dot(hidden, w_down[0], preferred_element_type=jnp.float32)
        if chunk == 0:
            sent_latent, partial_forward = lax.optimization_barrier(
                (sent_latent, partial_forward)
            )
        part = part + partner_sum(partial_forward)
        latent = layer_norm(part, norm_gain[2 * LAYERS], norm_bias[2 * LAYERS]).astype(jnp.bfloat16)
        if chunk == 1:
            sent_latent = latent
        else:
            own_latent = latent
    arrived_latent = from_behind(sent_latent, "tile", 1)
    later = (tile_index > 0).astype(jnp.float32)
    half_side = side // 2
    piece_planes = half_side // 2
    piece_tokens = piece_planes * side * side
    pieces = []
    gate = None
    for piece in range(half_side // piece_planes):
        span = slice(piece * piece_tokens, (piece + 1) * piece_tokens)
        latents = (own_latent[span], arrived_latent[span])
        if gate is not None:
            gate, latents = lax.optimization_barrier((gate, latents))
        lower_piece, upper_piece = [
            lax.dot_general(
                latent, decode_by_depth, (((1,), (2,)), ((), ())),
                preferred_element_type=jnp.float32,
            ).astype(jnp.bfloat16)
            for latent in latents
        ]
        shape = lower_piece.shape
        token_a = lax.broadcasted_iota(jnp.int32, shape, 0) // (side * side) + piece * piece_planes
        inner = lax.broadcasted_iota(jnp.int32, shape, 2) // PATCH
        places = (token_a * PATCH + head_index * inner_rows + inner).astype(jnp.float32)
        lower_profile = profile_of(places)
        upper_profile = profile_of(places + HALF)
        numerator = (
            lower_piece.astype(jnp.float32) * lower_profile
            + upper_piece.astype(jnp.float32) * upper_profile
        )
        denominator = lower_profile + later * upper_profile
        blended = (numerator / denominator).astype(jnp.bfloat16)
        arranged = blended.reshape(piece_planes * side, WIN, cell_cols)
        arranged = jnp.swapaxes(arranged, 1, 2).reshape(piece_planes, side, inner_rows, PATCH, WIN)
        gate = arranged
        other_rows = lax.ppermute(arranged, "head", [(0, 1), (1, 0)])
        whole = jnp.where(
            head_index == 0,
            jnp.concatenate([arranged, other_rows], 2),
            jnp.concatenate([other_rows, arranged], 2),
        )
        pieces.append(whole.transpose(0, 2, 1, 3, 4).reshape(piece_planes * PATCH, WIN, WIN))
    return jnp.concatenate(pieces, 0)


def solution(mesh):
    return jax.shard_map(
        body,
        mesh=mesh,
        in_specs=(
            P("tile", None, None),
            P("tile", None),
            P(None, "head"),
            P(None, "head"),
            P(None, "head"),
            P(),
            P(),
            P(None, None, None, "head"),
            P(None, "head", None),
            P(None, None, "head"),
            P(None, "head", None),
            P(None, "head"),
        ),
        out_specs=P("tile", None, None),
        check_vma=False,
    )
```

```python
import jax
import jax.numpy as jnp
from jax import lax
from jax.sharding import PartitionSpec as P

PATCH = 16
LAYERS = 1
WIN = 128
HEAD_DIM = 64
HALF = 64


EPSILON = 1e-06


def from_behind(block, axis, distance):
    devices = range(lax.axis_size(axis))
    route = [(i - distance, i) for i in devices if i - distance in devices]
    return lax.ppermute(block, axis, route)


def partner_sum(term):
    rounded = term.astype(jnp.bfloat16)
    other = lax.ppermute(rounded, "head", [(0, 1), (1, 0)])
    return rounded.astype(jnp.float32) + other.astype(jnp.float32)


def layer_norm(values, gain, bias):
    average = jnp.mean(values, axis=-1, keepdims=True)
    centered = values - average
    variance = jnp.mean(centered * centered, axis=-1, keepdims=True)
    return centered * lax.rsqrt(variance + EPSILON) * gain + bias


def profile_of(places):
    return jnp.exp(-0.5 * ((places - (WIN - 1) / 2) / (WIN / 4)) ** 2)


def embed_planes(amplitudes, live, embed_by_depth, embed_mask):
    side = WIN // PATCH
    depth_side = amplitudes.shape[0] // PATCH
    rows = depth_side * side * side
    masked = amplitudes * live[:, :, None]
    grouped = masked.reshape(depth_side, PATCH, side, PATCH, WIN).transpose(0, 2, 1, 3, 4)
    grouped = grouped.reshape(depth_side * side, PATCH * PATCH, WIN)
    voxels = jnp.swapaxes(grouped, 1, 2).reshape(rows, PATCH, PATCH * PATCH)
    embedded = lax.dot_general(
        voxels, embed_by_depth, (((1, 2), (0, 1)), ((), ())),
        preferred_element_type=jnp.float32,
    )
    mask_patches = (
        live.reshape(depth_side, PATCH, side, PATCH)
        .transpose(0, 2, 1, 3)
        .reshape(depth_side * side, PATCH * PATCH)
    )
    mask_terms = jnp.dot(mask_patches, embed_mask, preferred_element_type=jnp.float32)
    local_width = mask_terms.shape[1]
    return embedded + jnp.broadcast_to(
        mask_terms[:, None, :], (depth_side * side, side, local_width)
    ).reshape(rows, local_width)


def body(
    traces,
    trace_mask,
    embed_voxel,
    embed_mask,
    position,
    norm_gain,
    norm_bias,
    w_qkv,
    w_out,
    w_up,
    w_down,
    w_decode,
):
    side = WIN // PATCH
    tokens = side**3
    half_tokens = tokens // 2
    tile_index = lax.axis_index("tile")
    head_index = lax.axis_index("head")
    own_live = trace_mask.astype(jnp.bfloat16)
    other_w_out = lax.ppermute(w_out[0], "head", [(0, 1), (1, 0)])
    local_width = embed_voxel.shape[1]
    embed_by_depth = embed_voxel.reshape(PATCH * PATCH, PATCH, local_width).transpose(1, 0, 2)
    position = position.astype(jnp.float32)
    own_embedded = embed_planes(traces, own_live, embed_by_depth, embed_mask)
    next_embedded = from_behind(own_embedded, "tile", -1)
    halves = []
    for rows, embedded in enumerate((own_embedded, next_embedded)):
        embedded = embedded + position[rows * half_tokens:(rows + 1) * half_tokens]
        embedded = embedded.astype(jnp.bfloat16)
        other_columns = lax.ppermute(embedded, "head", [(0, 1), (1, 0)])
        halves.append(jnp.where(
            head_index == 0,
            jnp.concatenate([embedded, other_columns], 1),
            jnp.concatenate([other_columns, embedded], 1),
        ).astype(jnp.float32))
    stream = jnp.concatenate(halves, 0)
    local_heads = w_qkv.shape[3] // HEAD_DIM
    normed = layer_norm(stream, norm_gain[0], norm_bias[0]).astype(jnp.bfloat16)
    projected = jnp.einsum(
        "td,sde->ste", normed, w_qkv[0], preferred_element_type=jnp.float32
    ).astype(jnp.bfloat16)
    keys = projected[1].reshape(tokens, local_heads, HEAD_DIM)
    values = projected[2].reshape(tokens, local_heads, HEAD_DIM)
    inner_rows = w_decode.shape[1] // (PATCH * PATCH)
    cell_cols = inner_rows * PATCH
    decode_by_depth = (
        w_decode.T.reshape(inner_rows, PATCH, PATCH, -1)
        .transpose(2, 0, 1, 3)
        .reshape(PATCH, cell_cols, -1)
    )
    for chunk in (1, 0):
        span = slice(chunk * half_tokens, (chunk + 1) * half_tokens)
        query = projected[0][span].reshape(half_tokens, local_heads, HEAD_DIM)
        scores = jnp.einsum(
            "thd,shd->hts", query, keys, preferred_element_type=jnp.float32
        ) * HEAD_DIM ** (-0.5)
        weights = jax.nn.softmax(scores, axis=-1).astype(jnp.bfloat16)
        attended = jnp.einsum(
            "hts,shd->thd", weights, values, preferred_element_type=jnp.float32
        ).astype(jnp.bfloat16)
        attended = attended.reshape(half_tokens, local_heads * HEAD_DIM)
        other_attended = lax.ppermute(attended, "head", [(0, 1), (1, 0)])
        own_term = jnp.dot(attended, w_out[0], preferred_element_type=jnp.float32)
        other_term = jnp.dot(other_attended, other_w_out, preferred_element_type=jnp.float32)
        part = stream[span] + (
            own_term.astype(jnp.bfloat16).astype(jnp.float32)
            + other_term.astype(jnp.bfloat16).astype(jnp.float32)
        )
        normed = layer_norm(part, norm_gain[1], norm_bias[1]).astype(jnp.bfloat16)
        hidden = jax.nn.gelu(
            jnp.dot(normed, w_up[0], preferred_element_type=jnp.float32), approximate=True
        ).astype(jnp.bfloat16)
        partial_forward = jnp.dot(hidden, w_down[0], preferred_element_type=jnp.float32)
        if chunk == 0:
            sent_latent, partial_forward = lax.optimization_barrier(
                (sent_latent, partial_forward)
            )
        part = part + partner_sum(partial_forward)
        latent = layer_norm(part, norm_gain[2 * LAYERS], norm_bias[2 * LAYERS]).astype(jnp.bfloat16)
        if chunk == 1:
            sent_latent = latent
        else:
            own_latent = latent
    arrived_latent = from_behind(sent_latent, "tile", 1)
    later = (tile_index > 0).astype(jnp.float32)
    half_side = side // 2
    piece_planes = half_side // 4
    piece_tokens = piece_planes * side * side
    pieces = []
    gate = None
    for piece in range(half_side // piece_planes):
        span = slice(piece * piece_tokens, (piece + 1) * piece_tokens)
        latents = (own_latent[span], arrived_latent[span])
        if gate is not None:
            gate, latents = lax.optimization_barrier((gate, latents))
        lower_piece, upper_piece = [
            lax.dot_general(
                latent, decode_by_depth, (((1,), (2,)), ((), ())),
                preferred_element_type=jnp.float32,
            ).astype(jnp.bfloat16)
            for latent in latents
        ]
        shape = lower_piece.shape
        token_a = lax.broadcasted_iota(jnp.int32, shape, 0) // (side * side) + piece * piece_planes
        inner = lax.broadcasted_iota(jnp.int32, shape, 2) // PATCH
        places = (token_a * PATCH + head_index * inner_rows + inner).astype(jnp.float32)
        lower_profile = profile_of(places)
        upper_profile = profile_of(places + HALF)
        numerator = (
            lower_piece.astype(jnp.float32) * lower_profile
            + upper_piece.astype(jnp.float32) * upper_profile
        )
        denominator = lower_profile + later * upper_profile
        blended = (numerator / denominator).astype(jnp.bfloat16)
        arranged = blended.reshape(piece_planes * side, WIN, cell_cols)
        arranged = jnp.swapaxes(arranged, 1, 2).reshape(piece_planes, side, inner_rows, PATCH, WIN)
        gate = arranged
        other_rows = lax.ppermute(arranged, "head", [(0, 1), (1, 0)])
        whole = jnp.where(
            head_index == 0,
            jnp.concatenate([arranged, other_rows], 2),
            jnp.concatenate([other_rows, arranged], 2),
        )
        pieces.append(whole.transpose(0, 2, 1, 3, 4).reshape(piece_planes * PATCH, WIN, WIN))
    return jnp.concatenate(pieces, 0)


def solution(mesh):
    return jax.shard_map(
        body,
        mesh=mesh,
        in_specs=(
            P("tile", None, None),
            P("tile", None),
            P(None, "head"),
            P(None, "head"),
            P(None, "head"),
            P(),
            P(),
            P(None, None, None, "head"),
            P(None, "head", None),
            P(None, None, "head"),
            P(None, "head", None),
            P(None, "head"),
        ),
        out_specs=P("tile", None, None),
        check_vma=False,
    )
```

```python
import jax
import jax.numpy as jnp
from jax import lax
from jax.sharding import PartitionSpec as P

PATCH = 16
LAYERS = 1
WIN = 128
HEAD_DIM = 64
HALF = 64


EPSILON = 1e-06


def from_behind(block, axis, distance):
    devices = range(lax.axis_size(axis))
    route = [(i - distance, i) for i in devices if i - distance in devices]
    return lax.ppermute(block, axis, route)


def partner_sum(term):
    rounded = term.astype(jnp.bfloat16)
    other = lax.ppermute(rounded, "head", [(0, 1), (1, 0)])
    return rounded.astype(jnp.float32) + other.astype(jnp.float32)


def layer_norm(values, gain, bias):
    average = jnp.mean(values, axis=-1, keepdims=True)
    centered = values - average
    variance = jnp.mean(centered * centered, axis=-1, keepdims=True)
    return centered * lax.rsqrt(variance + EPSILON) * gain + bias


def profile_of(places):
    return jnp.exp(-0.5 * ((places - (WIN - 1) / 2) / (WIN / 4)) ** 2)


def embed_planes(amplitudes, live, embed_by_depth, embed_mask):
    side = WIN // PATCH
    depth_side = amplitudes.shape[0] // PATCH
    rows = depth_side * side * side
    masked = amplitudes * live[:, :, None]
    grouped = masked.reshape(depth_side, PATCH, side, PATCH, WIN).transpose(0, 2, 1, 3, 4)
    grouped = grouped.reshape(depth_side * side, PATCH * PATCH, WIN)
    voxels = jnp.swapaxes(grouped, 1, 2).reshape(rows, PATCH, PATCH * PATCH)
    embedded = lax.dot_general(
        voxels, embed_by_depth, (((1, 2), (0, 1)), ((), ())),
        preferred_element_type=jnp.float32,
    )
    mask_patches = (
        live.reshape(depth_side, PATCH, side, PATCH)
        .transpose(0, 2, 1, 3)
        .reshape(depth_side * side, PATCH * PATCH)
    )
    mask_terms = jnp.dot(mask_patches, embed_mask, preferred_element_type=jnp.float32)
    local_width = mask_terms.shape[1]
    return embedded + jnp.broadcast_to(
        mask_terms[:, None, :], (depth_side * side, side, local_width)
    ).reshape(rows, local_width)


def body(
    traces,
    trace_mask,
    embed_voxel,
    embed_mask,
    position,
    norm_gain,
    norm_bias,
    w_qkv,
    w_out,
    w_up,
    w_down,
    w_decode,
):
    side = WIN // PATCH
    tokens = side**3
    half_tokens = tokens // 2
    tile_index = lax.axis_index("tile")
    head_index = lax.axis_index("head")
    own_live = trace_mask.astype(jnp.bfloat16)
    other_w_out = lax.ppermute(w_out[0], "head", [(0, 1), (1, 0)])
    local_width = embed_voxel.shape[1]
    embed_by_depth = embed_voxel.reshape(PATCH * PATCH, PATCH, local_width).transpose(1, 0, 2)
    position = position.astype(jnp.float32)
    own_embedded = embed_planes(traces, own_live, embed_by_depth, embed_mask)
    own_half = (own_embedded + position[:half_tokens]).astype(jnp.bfloat16)
    for_previous = (own_embedded + position[half_tokens:]).astype(jnp.bfloat16)
    next_half = jnp.where(
        tile_index == lax.axis_size("tile") - 1,
        position[half_tokens:].astype(jnp.bfloat16),
        from_behind(for_previous, "tile", -1),
    )
    halves = []
    for embedded in (own_half, next_half):
        other_columns = lax.ppermute(embedded, "head", [(0, 1), (1, 0)])
        halves.append(jnp.where(
            head_index == 0,
            jnp.concatenate([embedded, other_columns], 1),
            jnp.concatenate([other_columns, embedded], 1),
        ).astype(jnp.float32))
    stream = jnp.concatenate(halves, 0)
    local_heads = w_qkv.shape[3] // HEAD_DIM
    normed = layer_norm(stream, norm_gain[0], norm_bias[0]).astype(jnp.bfloat16)
    projected = jnp.einsum(
        "td,sde->ste", normed, w_qkv[0], preferred_element_type=jnp.float32
    ).astype(jnp.bfloat16)
    keys = projected[1].reshape(tokens, local_heads, HEAD_DIM)
    values = projected[2].reshape(tokens, local_heads, HEAD_DIM)
    inner_rows = w_decode.shape[1] // (PATCH * PATCH)
    cell_cols = inner_rows * PATCH
    decode_by_depth = (
        w_decode.T.reshape(inner_rows, PATCH, PATCH, -1)
        .transpose(2, 0, 1, 3)
        .reshape(PATCH, cell_cols, -1)
    )
    for chunk in (1, 0):
        span = slice(chunk * half_tokens, (chunk + 1) * half_tokens)
        query = projected[0][span].reshape(half_tokens, local_heads, HEAD_DIM)
        scores = jnp.einsum(
            "thd,shd->hts", query, keys, preferred_element_type=jnp.float32
        ) * HEAD_DIM ** (-0.5)
        weights = jax.nn.softmax(scores, axis=-1).astype(jnp.bfloat16)
        attended = jnp.einsum(
            "hts,shd->thd", weights, values, preferred_element_type=jnp.float32
        ).astype(jnp.bfloat16)
        attended = attended.reshape(half_tokens, local_heads * HEAD_DIM)
        other_attended = lax.ppermute(attended, "head", [(0, 1), (1, 0)])
        own_term = jnp.dot(attended, w_out[0], preferred_element_type=jnp.float32)
        other_term = jnp.dot(other_attended, other_w_out, preferred_element_type=jnp.float32)
        part = stream[span] + (
            own_term.astype(jnp.bfloat16).astype(jnp.float32)
            + other_term.astype(jnp.bfloat16).astype(jnp.float32)
        )
        normed = layer_norm(part, norm_gain[1], norm_bias[1]).astype(jnp.bfloat16)
        hidden = jax.nn.gelu(
            jnp.dot(normed, w_up[0], preferred_element_type=jnp.float32), approximate=True
        ).astype(jnp.bfloat16)
        partial_forward = jnp.dot(hidden, w_down[0], preferred_element_type=jnp.float32)
        if chunk == 0:
            sent_latent, partial_forward = lax.optimization_barrier(
                (sent_latent, partial_forward)
            )
        part = part + partner_sum(partial_forward)
        latent = layer_norm(part, norm_gain[2 * LAYERS], norm_bias[2 * LAYERS]).astype(jnp.bfloat16)
        if chunk == 1:
            sent_latent = latent
        else:
            own_latent = latent
    arrived_latent = from_behind(sent_latent, "tile", 1)
    later = (tile_index > 0).astype(jnp.float32)
    half_side = side // 2
    piece_planes = half_side // 2
    piece_tokens = piece_planes * side * side
    pieces = []
    gate = None
    for piece in range(half_side // piece_planes):
        span = slice(piece * piece_tokens, (piece + 1) * piece_tokens)
        latents = (own_latent[span], arrived_latent[span])
        if gate is not None:
            gate, latents = lax.optimization_barrier((gate, latents))
        lower_piece, upper_piece = [
            lax.dot_general(
                latent, decode_by_depth, (((1,), (2,)), ((), ())),
                preferred_element_type=jnp.float32,
            ).astype(jnp.bfloat16)
            for latent in latents
        ]
        shape = lower_piece.shape
        token_a = lax.broadcasted_iota(jnp.int32, shape, 0) // (side * side) + piece * piece_planes
        inner = lax.broadcasted_iota(jnp.int32, shape, 2) // PATCH
        places = (token_a * PATCH + head_index * inner_rows + inner).astype(jnp.float32)
        lower_profile = profile_of(places)
        upper_profile = profile_of(places + HALF)
        numerator = (
            lower_piece.astype(jnp.float32) * lower_profile
            + upper_piece.astype(jnp.float32) * upper_profile
        )
        denominator = lower_profile + later * upper_profile
        blended = (numerator / denominator).astype(jnp.bfloat16)
        arranged = blended.reshape(piece_planes * side, WIN, cell_cols)
        arranged = jnp.swapaxes(arranged, 1, 2).reshape(piece_planes, side, inner_rows, PATCH, WIN)
        gate = arranged
        other_rows = lax.ppermute(arranged, "head", [(0, 1), (1, 0)])
        whole = jnp.where(
            head_index == 0,
            jnp.concatenate([arranged, other_rows], 2),
            jnp.concatenate([other_rows, arranged], 2),
        )
        pieces.append(whole.transpose(0, 2, 1, 3, 4).reshape(piece_planes * PATCH, WIN, WIN))
    return jnp.concatenate(pieces, 0)


def solution(mesh):
    return jax.shard_map(
        body,
        mesh=mesh,
        in_specs=(
            P("tile", None, None),
            P("tile", None),
            P(None, "head"),
            P(None, "head"),
            P(None, "head"),
            P(),
            P(),
            P(None, None, None, "head"),
            P(None, "head", None),
            P(None, None, "head"),
            P(None, "head", None),
            P(None, "head"),
        ),
        out_specs=P("tile", None, None),
        check_vma=False,
    )
```

```python
import jax
import jax.numpy as jnp
from jax import lax
from jax.sharding import PartitionSpec as P

PATCH = 16
LAYERS = 1
WIN = 128
HEAD_DIM = 64
HALF = 64


EPSILON = 1e-06


def from_behind(block, axis, distance):
    devices = range(lax.axis_size(axis))
    route = [(i - distance, i) for i in devices if i - distance in devices]
    return lax.ppermute(block, axis, route)


def partner_sum(term):
    rounded = term.astype(jnp.bfloat16)
    other = lax.ppermute(rounded, "head", [(0, 1), (1, 0)])
    return rounded.astype(jnp.float32) + other.astype(jnp.float32)


def layer_norm(values, gain, bias):
    average = jnp.mean(values, axis=-1, keepdims=True)
    centered = values - average
    variance = jnp.mean(centered * centered, axis=-1, keepdims=True)
    return centered * lax.rsqrt(variance + EPSILON) * gain + bias


def profile_of(places):
    return jnp.exp(-0.5 * ((places - (WIN - 1) / 2) / (WIN / 4)) ** 2)


def embed_planes(amplitudes, live, embed_by_depth, embed_mask):
    side = WIN // PATCH
    depth_side = amplitudes.shape[0] // PATCH
    rows = depth_side * side * side
    masked = amplitudes * live[:, :, None]
    grouped = masked.reshape(depth_side, PATCH, side, PATCH, WIN).transpose(0, 2, 1, 3, 4)
    grouped = grouped.reshape(depth_side * side, PATCH * PATCH, WIN)
    voxels = jnp.swapaxes(grouped, 1, 2).reshape(rows, PATCH, PATCH * PATCH)
    embedded = lax.dot_general(
        voxels, embed_by_depth, (((1, 2), (0, 1)), ((), ())),
        preferred_element_type=jnp.float32,
    )
    mask_patches = (
        live.reshape(depth_side, PATCH, side, PATCH)
        .transpose(0, 2, 1, 3)
        .reshape(depth_side * side, PATCH * PATCH)
    )
    mask_terms = jnp.dot(mask_patches, embed_mask, preferred_element_type=jnp.float32)
    local_width = mask_terms.shape[1]
    return embedded + jnp.broadcast_to(
        mask_terms[:, None, :], (depth_side * side, side, local_width)
    ).reshape(rows, local_width)


def body(
    traces,
    trace_mask,
    embed_voxel,
    embed_mask,
    position,
    norm_gain,
    norm_bias,
    w_qkv,
    w_out,
    w_up,
    w_down,
    w_decode,
):
    side = WIN // PATCH
    tokens = side**3
    half_tokens = tokens // 2
    tile_index = lax.axis_index("tile")
    head_index = lax.axis_index("head")
    own_live = trace_mask.astype(jnp.bfloat16)
    other_w_out = lax.ppermute(w_out[0], "head", [(0, 1), (1, 0)])
    local_width = embed_voxel.shape[1]
    embed_by_depth = embed_voxel.reshape(PATCH * PATCH, PATCH, local_width).transpose(1, 0, 2)
    position = position.astype(jnp.float32)
    own_embedded = embed_planes(traces, own_live, embed_by_depth, embed_mask)
    own_half = (own_embedded + position[:half_tokens]).astype(jnp.bfloat16)
    for_previous = (own_embedded + position[half_tokens:]).astype(jnp.bfloat16)
    next_half = jnp.where(
        tile_index == lax.axis_size("tile") - 1,
        position[half_tokens:].astype(jnp.bfloat16),
        from_behind(for_previous, "tile", -1),
    )
    halves = []
    for embedded in (own_half, next_half):
        other_columns = lax.ppermute(embedded, "head", [(0, 1), (1, 0)])
        halves.append(jnp.where(
            head_index == 0,
            jnp.concatenate([embedded, other_columns], 1),
            jnp.concatenate([other_columns, embedded], 1),
        ).astype(jnp.float32))
    stream = jnp.concatenate(halves, 0)
    local_heads = w_qkv.shape[3] // HEAD_DIM
    normed = layer_norm(stream, norm_gain[0], norm_bias[0]).astype(jnp.bfloat16)
    projected = jnp.einsum(
        "td,sde->ste", normed, w_qkv[0], preferred_element_type=jnp.float32
    ).astype(jnp.bfloat16)
    keys = projected[1].reshape(tokens, local_heads, HEAD_DIM)
    values = projected[2].reshape(tokens, local_heads, HEAD_DIM)
    inner_rows = w_decode.shape[1] // (PATCH * PATCH)
    cell_cols = inner_rows * PATCH
    decode_by_depth = (
        w_decode.T.reshape(inner_rows, PATCH, PATCH, -1)
        .transpose(2, 0, 1, 3)
        .reshape(PATCH, cell_cols, -1)
    )
    for chunk in (1, 0):
        span = slice(chunk * half_tokens, (chunk + 1) * half_tokens)
        query = projected[0][span].reshape(half_tokens, local_heads, HEAD_DIM)
        scores = jnp.einsum(
            "thd,shd->hts", query, keys, preferred_element_type=jnp.float32
        ) * HEAD_DIM ** (-0.5)
        weights = jax.nn.softmax(scores, axis=-1).astype(jnp.bfloat16)
        attended = jnp.einsum(
            "hts,shd->thd", weights, values, preferred_element_type=jnp.float32
        ).astype(jnp.bfloat16)
        attended = attended.reshape(half_tokens, local_heads * HEAD_DIM)
        other_attended = lax.ppermute(attended, "head", [(0, 1), (1, 0)])
        own_term = jnp.dot(attended, w_out[0], preferred_element_type=jnp.float32)
        other_term = jnp.dot(other_attended, other_w_out, preferred_element_type=jnp.float32)
        part = stream[span] + (
            own_term.astype(jnp.bfloat16).astype(jnp.float32)
            + other_term.astype(jnp.bfloat16).astype(jnp.float32)
        )
        normed = layer_norm(part, norm_gain[1], norm_bias[1]).astype(jnp.bfloat16)
        hidden = jax.nn.gelu(
            jnp.dot(normed, w_up[0], preferred_element_type=jnp.float32), approximate=True
        ).astype(jnp.bfloat16)
        partial_forward = jnp.dot(hidden, w_down[0], preferred_element_type=jnp.float32)
        if chunk == 0:
            sent_latent, partial_forward = lax.optimization_barrier(
                (sent_latent, partial_forward)
            )
        if chunk == 1:
            part = part + partner_sum(partial_forward)
            sent_latent = layer_norm(
                part, norm_gain[2 * LAYERS], norm_bias[2 * LAYERS]
            ).astype(jnp.bfloat16)
            continue
        latents = []
        piece_rows = half_tokens // 2
        for rows in range(0, half_tokens, piece_rows):
            piece = part[rows:rows + piece_rows] + partner_sum(partial_forward[rows:rows + piece_rows])
            latents.append(layer_norm(
                piece, norm_gain[2 * LAYERS], norm_bias[2 * LAYERS]
            ).astype(jnp.bfloat16))
        own_latent = jnp.concatenate(latents, 0)
    arrived_latent = from_behind(sent_latent, "tile", 1)
    later = (tile_index > 0).astype(jnp.float32)
    half_side = side // 2
    piece_planes = half_side // 2
    piece_tokens = piece_planes * side * side
    pieces = []
    gate = None
    for piece in range(half_side // piece_planes):
        span = slice(piece * piece_tokens, (piece + 1) * piece_tokens)
        latents = (own_latent[span], arrived_latent[span])
        if gate is not None:
            gate, latents = lax.optimization_barrier((gate, latents))
        lower_piece, upper_piece = [
            lax.dot_general(
                latent, decode_by_depth, (((1,), (2,)), ((), ())),
                preferred_element_type=jnp.float32,
            ).astype(jnp.bfloat16)
            for latent in latents
        ]
        shape = lower_piece.shape
        token_a = lax.broadcasted_iota(jnp.int32, shape, 0) // (side * side) + piece * piece_planes
        inner = lax.broadcasted_iota(jnp.int32, shape, 2) // PATCH
        places = (token_a * PATCH + head_index * inner_rows + inner).astype(jnp.float32)
        lower_profile = profile_of(places)
        upper_profile = profile_of(places + HALF)
        numerator = (
            lower_piece.astype(jnp.float32) * lower_profile
            + upper_piece.astype(jnp.float32) * upper_profile
        )
        denominator = lower_profile + later * upper_profile
        blended = (numerator / denominator).astype(jnp.bfloat16)
        arranged = blended.reshape(piece_planes * side, WIN, cell_cols)
        arranged = jnp.swapaxes(arranged, 1, 2).reshape(piece_planes, side, inner_rows, PATCH, WIN)
        gate = arranged
        other_rows = lax.ppermute(arranged, "head", [(0, 1), (1, 0)])
        whole = jnp.where(
            head_index == 0,
            jnp.concatenate([arranged, other_rows], 2),
            jnp.concatenate([other_rows, arranged], 2),
        )
        pieces.append(whole.transpose(0, 2, 1, 3, 4).reshape(piece_planes * PATCH, WIN, WIN))
    return jnp.concatenate(pieces, 0)


def solution(mesh):
    return jax.shard_map(
        body,
        mesh=mesh,
        in_specs=(
            P("tile", None, None),
            P("tile", None),
            P(None, "head"),
            P(None, "head"),
            P(None, "head"),
            P(),
            P(),
            P(None, None, None, "head"),
            P(None, "head", None),
            P(None, None, "head"),
            P(None, "head", None),
            P(None, "head"),
        ),
        out_specs=P("tile", None, None),
        check_vma=False,
    )
```

```python
import jax
import jax.numpy as jnp
from jax import lax
from jax.sharding import PartitionSpec as P

PATCH = 16
LAYERS = 1
WIN = 128
HEAD_DIM = 64
HALF = 64


EPSILON = 1e-06


def from_behind(block, axis, distance):
    devices = range(lax.axis_size(axis))
    route = [(i - distance, i) for i in devices if i - distance in devices]
    return lax.ppermute(block, axis, route)


def partner_sum(term):
    rounded = term.astype(jnp.bfloat16)
    other = lax.ppermute(rounded, "head", [(0, 1), (1, 0)])
    return rounded.astype(jnp.float32) + other.astype(jnp.float32)


def layer_norm(values, gain, bias):
    average = jnp.mean(values, axis=-1, keepdims=True)
    centered = values - average
    variance = jnp.mean(centered * centered, axis=-1, keepdims=True)
    return centered * lax.rsqrt(variance + EPSILON) * gain + bias


def profile_of(places):
    return jnp.exp(-0.5 * ((places - (WIN - 1) / 2) / (WIN / 4)) ** 2)


def embed_planes(amplitudes, live, embed_by_depth, embed_mask):
    side = WIN // PATCH
    depth_side = amplitudes.shape[0] // PATCH
    rows = depth_side * side * side
    masked = amplitudes * live[:, :, None]
    grouped = masked.reshape(depth_side, PATCH, side, PATCH, WIN).transpose(0, 2, 1, 3, 4)
    grouped = grouped.reshape(depth_side * side, PATCH * PATCH, WIN)
    voxels = jnp.swapaxes(grouped, 1, 2).reshape(rows, PATCH, PATCH * PATCH)
    embedded = lax.dot_general(
        voxels, embed_by_depth, (((1, 2), (0, 1)), ((), ())),
        preferred_element_type=jnp.float32,
    )
    mask_patches = (
        live.reshape(depth_side, PATCH, side, PATCH)
        .transpose(0, 2, 1, 3)
        .reshape(depth_side * side, PATCH * PATCH)
    )
    mask_terms = jnp.dot(mask_patches, embed_mask, preferred_element_type=jnp.float32)
    local_width = mask_terms.shape[1]
    return embedded + jnp.broadcast_to(
        mask_terms[:, None, :], (depth_side * side, side, local_width)
    ).reshape(rows, local_width)


def body(
    traces,
    trace_mask,
    embed_voxel,
    embed_mask,
    position,
    norm_gain,
    norm_bias,
    w_qkv,
    w_out,
    w_up,
    w_down,
    w_decode,
):
    side = WIN // PATCH
    tokens = side**3
    half_tokens = tokens // 2
    tile_index = lax.axis_index("tile")
    head_index = lax.axis_index("head")
    own_live = trace_mask.astype(jnp.bfloat16)
    tile_count = lax.axis_size("tile")
    devices = 2 * tile_count
    across = [(index, index ^ (tile_count + 1)) for index in range(devices)]
    other_w_decode = lax.ppermute(w_decode, ("tile", "head"), across)
    other_w_out = lax.ppermute(w_out[0], "head", [(0, 1), (1, 0)])
    local_width = embed_voxel.shape[1]
    embed_by_depth = embed_voxel.reshape(PATCH * PATCH, PATCH, local_width).transpose(1, 0, 2)
    position = position.astype(jnp.float32)
    own_embedded = embed_planes(traces, own_live, embed_by_depth, embed_mask)
    own_half = (own_embedded + position[:half_tokens]).astype(jnp.bfloat16)
    for_previous = (own_embedded + position[half_tokens:]).astype(jnp.bfloat16)
    next_half = jnp.where(
        tile_index == lax.axis_size("tile") - 1,
        position[half_tokens:].astype(jnp.bfloat16),
        from_behind(for_previous, "tile", -1),
    )
    halves = []
    for embedded in (own_half, next_half):
        other_columns = lax.ppermute(embedded, "head", [(0, 1), (1, 0)])
        halves.append(jnp.where(
            head_index == 0,
            jnp.concatenate([embedded, other_columns], 1),
            jnp.concatenate([other_columns, embedded], 1),
        ).astype(jnp.float32))
    stream = jnp.concatenate(halves, 0)
    local_heads = w_qkv.shape[3] // HEAD_DIM
    normed = layer_norm(stream, norm_gain[0], norm_bias[0]).astype(jnp.bfloat16)
    projected = jnp.einsum(
        "td,sde->ste", normed, w_qkv[0], preferred_element_type=jnp.float32
    ).astype(jnp.bfloat16)
    keys = projected[1].reshape(tokens, local_heads, HEAD_DIM)
    values = projected[2].reshape(tokens, local_heads, HEAD_DIM)
    whole_w_decode = jnp.where(
        head_index == 0,
        jnp.concatenate([w_decode, other_w_decode], 1),
        jnp.concatenate([other_w_decode, w_decode], 1),
    )
    inner_rows = PATCH
    cell_cols = inner_rows * PATCH
    decode_by_depth = (
        whole_w_decode.T.reshape(inner_rows, PATCH, PATCH, -1)
        .transpose(2, 0, 1, 3)
        .reshape(PATCH, cell_cols, -1)
    )
    for chunk in (1, 0):
        span = slice(chunk * half_tokens, (chunk + 1) * half_tokens)
        query = projected[0][span].reshape(half_tokens, local_heads, HEAD_DIM)
        scores = jnp.einsum(
            "thd,shd->hts", query, keys, preferred_element_type=jnp.float32
        ) * HEAD_DIM ** (-0.5)
        weights = jax.nn.softmax(scores, axis=-1).astype(jnp.bfloat16)
        attended = jnp.einsum(
            "hts,shd->thd", weights, values, preferred_element_type=jnp.float32
        ).astype(jnp.bfloat16)
        attended = attended.reshape(half_tokens, local_heads * HEAD_DIM)
        other_attended = lax.ppermute(attended, "head", [(0, 1), (1, 0)])
        own_term = jnp.dot(attended, w_out[0], preferred_element_type=jnp.float32)
        other_term = jnp.dot(other_attended, other_w_out, preferred_element_type=jnp.float32)
        part = stream[span] + (
            own_term.astype(jnp.bfloat16).astype(jnp.float32)
            + other_term.astype(jnp.bfloat16).astype(jnp.float32)
        )
        normed = layer_norm(part, norm_gain[1], norm_bias[1]).astype(jnp.bfloat16)
        hidden = jax.nn.gelu(
            jnp.dot(normed, w_up[0], preferred_element_type=jnp.float32), approximate=True
        ).astype(jnp.bfloat16)
        partial_forward = jnp.dot(hidden, w_down[0], preferred_element_type=jnp.float32)
        if chunk == 0:
            sent_latent, partial_forward = lax.optimization_barrier(
                (sent_latent, partial_forward)
            )
        part = part + partner_sum(partial_forward)
        latent = layer_norm(part, norm_gain[2 * LAYERS], norm_bias[2 * LAYERS]).astype(jnp.bfloat16)
        if chunk == 1:
            sent_latent = latent
        else:
            own_latent = latent
    arrived_latent = from_behind(sent_latent, "tile", 1)
    later = (tile_index > 0).astype(jnp.float32)
    half_side = side // 2
    lower_piece, upper_piece = [
        lax.dot_general(
            latent, decode_by_depth, (((1,), (2,)), ((), ())),
            preferred_element_type=jnp.float32,
        ).astype(jnp.bfloat16)
        for latent in (own_latent, arrived_latent)
    ]
    shape = lower_piece.shape
    token_a = lax.broadcasted_iota(jnp.int32, shape, 0) // (side * side)
    inner = lax.broadcasted_iota(jnp.int32, shape, 2) // PATCH
    places = (token_a * PATCH + inner).astype(jnp.float32)
    lower_profile = profile_of(places)
    upper_profile = profile_of(places + HALF)
    numerator = (
        lower_piece.astype(jnp.float32) * lower_profile
        + upper_piece.astype(jnp.float32) * upper_profile
    )
    denominator = lower_profile + later * upper_profile
    blended = (numerator / denominator).astype(jnp.bfloat16)
    arranged = blended.reshape(half_side * side, WIN, cell_cols)
    arranged = jnp.swapaxes(arranged, 1, 2).reshape(half_side, side, PATCH, PATCH, WIN)
    return arranged.transpose(0, 2, 1, 3, 4).reshape(HALF, WIN, WIN)


def solution(mesh):
    return jax.shard_map(
        body,
        mesh=mesh,
        in_specs=(
            P("tile", None, None),
            P("tile", None),
            P(None, "head"),
            P(None, "head"),
            P(None, "head"),
            P(),
            P(),
            P(None, None, None, "head"),
            P(None, "head", None),
            P(None, None, "head"),
            P(None, "head", None),
            P(None, "head"),
        ),
        out_specs=P("tile", None, None),
        check_vma=False,
    )
```

```python
import jax
import jax.numpy as jnp
from jax import lax
from jax.sharding import PartitionSpec as P

PATCH = 16
LAYERS = 1
WIN = 128
HEAD_DIM = 64
HALF = 64


EPSILON = 1e-06


def from_behind(block, axis, distance):
    devices = range(lax.axis_size(axis))
    route = [(i - distance, i) for i in devices if i - distance in devices]
    return lax.ppermute(block, axis, route)


def partner_sum(term):
    rounded = term.astype(jnp.bfloat16)
    other = lax.ppermute(rounded, "head", [(0, 1), (1, 0)])
    return rounded.astype(jnp.float32) + other.astype(jnp.float32)


def layer_norm(values, gain, bias):
    average = jnp.mean(values, axis=-1, keepdims=True)
    centered = values - average
    variance = jnp.mean(centered * centered, axis=-1, keepdims=True)
    return centered * lax.rsqrt(variance + EPSILON) * gain + bias


def profile_of(places):
    return jnp.exp(-0.5 * ((places - (WIN - 1) / 2) / (WIN / 4)) ** 2)


def embed_planes(amplitudes, live, embed_by_depth, embed_mask):
    side = WIN // PATCH
    depth_side = amplitudes.shape[0] // PATCH
    rows = depth_side * side * side
    masked = amplitudes * live[:, :, None]
    grouped = masked.reshape(depth_side, PATCH, side, PATCH, WIN).transpose(0, 2, 1, 3, 4)
    grouped = grouped.reshape(depth_side * side, PATCH * PATCH, WIN)
    voxels = jnp.swapaxes(grouped, 1, 2).reshape(rows, PATCH, PATCH * PATCH)
    embedded = lax.dot_general(
        voxels, embed_by_depth, (((1, 2), (0, 1)), ((), ())),
        preferred_element_type=jnp.float32,
    )
    mask_patches = (
        live.reshape(depth_side, PATCH, side, PATCH)
        .transpose(0, 2, 1, 3)
        .reshape(depth_side * side, PATCH * PATCH)
    )
    mask_terms = jnp.dot(mask_patches, embed_mask, preferred_element_type=jnp.float32)
    local_width = mask_terms.shape[1]
    return embedded + jnp.broadcast_to(
        mask_terms[:, None, :], (depth_side * side, side, local_width)
    ).reshape(rows, local_width)


def body(
    traces,
    trace_mask,
    embed_voxel,
    embed_mask,
    position,
    norm_gain,
    norm_bias,
    w_qkv,
    w_out,
    w_up,
    w_down,
    w_decode,
):
    side = WIN // PATCH
    tokens = side**3
    half_tokens = tokens // 2
    tile_index = lax.axis_index("tile")
    head_index = lax.axis_index("head")
    own_live = trace_mask.astype(jnp.bfloat16)
    tile_count = lax.axis_size("tile")
    devices = 2 * tile_count
    across = [(index, index ^ (tile_count + 1)) for index in range(devices)]
    other_w_decode = lax.ppermute(w_decode, ("tile", "head"), across)
    other_w_out = lax.ppermute(w_out[0], "head", [(0, 1), (1, 0)])
    local_width = embed_voxel.shape[1]
    embed_by_depth = embed_voxel.reshape(PATCH * PATCH, PATCH, local_width).transpose(1, 0, 2)
    position = position.astype(jnp.float32)
    own_embedded = embed_planes(traces, own_live, embed_by_depth, embed_mask)
    own_half = (own_embedded + position[:half_tokens]).astype(jnp.bfloat16)
    for_previous = (own_embedded + position[half_tokens:]).astype(jnp.bfloat16)
    next_half = jnp.where(
        tile_index == lax.axis_size("tile") - 1,
        position[half_tokens:].astype(jnp.bfloat16),
        from_behind(for_previous, "tile", -1),
    )
    halves = []
    for embedded in (own_half, next_half):
        other_columns = lax.ppermute(embedded, "head", [(0, 1), (1, 0)])
        halves.append(jnp.where(
            head_index == 0,
            jnp.concatenate([embedded, other_columns], 1),
            jnp.concatenate([other_columns, embedded], 1),
        ).astype(jnp.float32))
    stream = jnp.concatenate(halves, 0)
    local_heads = w_qkv.shape[3] // HEAD_DIM
    normed = layer_norm(stream, norm_gain[0], norm_bias[0]).astype(jnp.bfloat16)
    projected = jnp.einsum(
        "td,sde->ste", normed, w_qkv[0], preferred_element_type=jnp.float32
    ).astype(jnp.bfloat16)
    keys = projected[1].reshape(tokens, local_heads, HEAD_DIM)
    values = projected[2].reshape(tokens, local_heads, HEAD_DIM)
    inner_rows = w_decode.shape[1] // (PATCH * PATCH)
    cell_cols = inner_rows * PATCH
    decode_by_depth = [
        columns.T.reshape(inner_rows, PATCH, PATCH, -1)
        .transpose(2, 0, 1, 3)
        .reshape(PATCH, cell_cols, -1)
        for columns in (w_decode, other_w_decode)
    ]
    for chunk in (1, 0):
        span = slice(chunk * half_tokens, (chunk + 1) * half_tokens)
        query = projected[0][span].reshape(half_tokens, local_heads, HEAD_DIM)
        scores = jnp.einsum(
            "thd,shd->hts", query, keys, preferred_element_type=jnp.float32
        ) * HEAD_DIM ** (-0.5)
        weights = jax.nn.softmax(scores, axis=-1).astype(jnp.bfloat16)
        attended = jnp.einsum(
            "hts,shd->thd", weights, values, preferred_element_type=jnp.float32
        ).astype(jnp.bfloat16)
        attended = attended.reshape(half_tokens, local_heads * HEAD_DIM)
        other_attended = lax.ppermute(attended, "head", [(0, 1), (1, 0)])
        own_term = jnp.dot(attended, w_out[0], preferred_element_type=jnp.float32)
        other_term = jnp.dot(other_attended, other_w_out, preferred_element_type=jnp.float32)
        part = stream[span] + (
            own_term.astype(jnp.bfloat16).astype(jnp.float32)
            + other_term.astype(jnp.bfloat16).astype(jnp.float32)
        )
        normed = layer_norm(part, norm_gain[1], norm_bias[1]).astype(jnp.bfloat16)
        hidden = jax.nn.gelu(
            jnp.dot(normed, w_up[0], preferred_element_type=jnp.float32), approximate=True
        ).astype(jnp.bfloat16)
        partial_forward = jnp.dot(hidden, w_down[0], preferred_element_type=jnp.float32)
        if chunk == 0:
            sent_latent, partial_forward = lax.optimization_barrier(
                (sent_latent, partial_forward)
            )
        part = part + partner_sum(partial_forward)
        latent = layer_norm(part, norm_gain[2 * LAYERS], norm_bias[2 * LAYERS]).astype(jnp.bfloat16)
        if chunk == 1:
            sent_latent = latent
        else:
            own_latent = latent
    arrived_latent = from_behind(sent_latent, "tile", 1)
    later = (tile_index > 0).astype(jnp.float32)
    half_side = side // 2
    arranged_halves = []
    for cells, first_row in zip(decode_by_depth, (head_index, 1 - head_index)):
        lower_piece, upper_piece = [
            lax.dot_general(
                latent, cells, (((1,), (2,)), ((), ())),
                preferred_element_type=jnp.float32,
            ).astype(jnp.bfloat16)
            for latent in (own_latent, arrived_latent)
        ]
        shape = lower_piece.shape
        token_a = lax.broadcasted_iota(jnp.int32, shape, 0) // (side * side)
        inner = lax.broadcasted_iota(jnp.int32, shape, 2) // PATCH
        places = (token_a * PATCH + first_row * inner_rows + inner).astype(jnp.float32)
        lower_profile = profile_of(places)
        upper_profile = profile_of(places + HALF)
        numerator = (
            lower_piece.astype(jnp.float32) * lower_profile
            + upper_piece.astype(jnp.float32) * upper_profile
        )
        denominator = lower_profile + later * upper_profile
        blended = (numerator / denominator).astype(jnp.bfloat16)
        arranged = blended.reshape(half_side * side, WIN, cell_cols)
        arranged_halves.append(
            jnp.swapaxes(arranged, 1, 2).reshape(half_side, side, inner_rows, PATCH, WIN)
        )
    own_rows, other_rows = arranged_halves
    whole = jnp.where(
        head_index == 0,
        jnp.concatenate([own_rows, other_rows], 2),
        jnp.concatenate([other_rows, own_rows], 2),
    )
    return whole.transpose(0, 2, 1, 3, 4).reshape(HALF, WIN, WIN)


def solution(mesh):
    return jax.shard_map(
        body,
        mesh=mesh,
        in_specs=(
            P("tile", None, None),
            P("tile", None),
            P(None, "head"),
            P(None, "head"),
            P(None, "head"),
            P(),
            P(),
            P(None, None, None, "head"),
            P(None, "head", None),
            P(None, None, "head"),
            P(None, "head", None),
            P(None, "head"),
        ),
        out_specs=P("tile", None, None),
        check_vma=False,
    )
```

```python
import jax
import jax.numpy as jnp
from jax import lax
from jax.sharding import PartitionSpec as P

PATCH = 16
LAYERS = 1
WIN = 128
HEAD_DIM = 64
HALF = 64


EPSILON = 1e-06


def from_behind(block, axis, distance):
    devices = range(lax.axis_size(axis))
    route = [(i - distance, i) for i in devices if i - distance in devices]
    return lax.ppermute(block, axis, route)


def partner_sum(term):
    rounded = term.astype(jnp.bfloat16)
    other = lax.ppermute(rounded, "head", [(0, 1), (1, 0)])
    return rounded.astype(jnp.float32) + other.astype(jnp.float32)


def layer_norm(values, gain, bias):
    average = jnp.mean(values, axis=-1, keepdims=True)
    centered = values - average
    variance = jnp.mean(centered * centered, axis=-1, keepdims=True)
    return centered * lax.rsqrt(variance + EPSILON) * gain + bias


def profile_of(places):
    return jnp.exp(-0.5 * ((places - (WIN - 1) / 2) / (WIN / 4)) ** 2)


def embed_planes(amplitudes, live, embed_by_depth, embed_mask):
    side = WIN // PATCH
    depth_side = amplitudes.shape[0] // PATCH
    rows = depth_side * side * side
    masked = amplitudes * live[:, :, None]
    grouped = masked.reshape(depth_side, PATCH, side, PATCH, WIN).transpose(0, 2, 1, 3, 4)
    grouped = grouped.reshape(depth_side * side, PATCH * PATCH, WIN)
    voxels = jnp.swapaxes(grouped, 1, 2).reshape(rows, PATCH, PATCH * PATCH)
    embedded = lax.dot_general(
        voxels, embed_by_depth, (((1, 2), (0, 1)), ((), ())),
        preferred_element_type=jnp.float32,
    )
    mask_patches = (
        live.reshape(depth_side, PATCH, side, PATCH)
        .transpose(0, 2, 1, 3)
        .reshape(depth_side * side, PATCH * PATCH)
    )
    mask_terms = jnp.dot(mask_patches, embed_mask, preferred_element_type=jnp.float32)
    local_width = mask_terms.shape[1]
    return embedded + jnp.broadcast_to(
        mask_terms[:, None, :], (depth_side * side, side, local_width)
    ).reshape(rows, local_width)


def body(
    traces,
    trace_mask,
    embed_voxel,
    embed_mask,
    position,
    norm_gain,
    norm_bias,
    w_qkv,
    w_out,
    w_up,
    w_down,
    w_decode,
):
    side = WIN // PATCH
    tokens = side**3
    half_tokens = tokens // 2
    tile_index = lax.axis_index("tile")
    head_index = lax.axis_index("head")
    own_live = trace_mask.astype(jnp.bfloat16)
    tile_count = lax.axis_size("tile")
    devices = 2 * tile_count
    across = [(index, index ^ (tile_count + 1)) for index in range(devices)]
    own_cells = w_decode.shape[1] // (PATCH * PATCH)
    own_by_depth = (
        w_decode.T.reshape(own_cells, PATCH, PATCH, -1)
        .transpose(2, 0, 1, 3)
        .reshape(PATCH, own_cells * PATCH, -1)
    )
    other_by_depth = lax.ppermute(own_by_depth, ("tile", "head"), across)
    other_w_out = lax.ppermute(w_out[0], "head", [(0, 1), (1, 0)])
    local_width = embed_voxel.shape[1]
    embed_by_depth = embed_voxel.reshape(PATCH * PATCH, PATCH, local_width).transpose(1, 0, 2)
    position = position.astype(jnp.float32)
    own_embedded = embed_planes(traces, own_live, embed_by_depth, embed_mask)
    own_half = (own_embedded + position[:half_tokens]).astype(jnp.bfloat16)
    for_previous = (own_embedded + position[half_tokens:]).astype(jnp.bfloat16)
    next_half = jnp.where(
        tile_index == lax.axis_size("tile") - 1,
        position[half_tokens:].astype(jnp.bfloat16),
        from_behind(for_previous, "tile", -1),
    )
    halves = []
    for embedded in (own_half, next_half):
        other_columns = lax.ppermute(embedded, "head", [(0, 1), (1, 0)])
        halves.append(jnp.where(
            head_index == 0,
            jnp.concatenate([embedded, other_columns], 1),
            jnp.concatenate([other_columns, embedded], 1),
        ).astype(jnp.float32))
    stream = jnp.concatenate(halves, 0)
    local_heads = w_qkv.shape[3] // HEAD_DIM
    normed = layer_norm(stream, norm_gain[0], norm_bias[0]).astype(jnp.bfloat16)
    projected = jnp.einsum(
        "td,sde->ste", normed, w_qkv[0], preferred_element_type=jnp.float32
    ).astype(jnp.bfloat16)
    keys = projected[1].reshape(tokens, local_heads, HEAD_DIM)
    values = projected[2].reshape(tokens, local_heads, HEAD_DIM)
    inner_rows = PATCH
    cell_cols = inner_rows * PATCH
    decode_by_depth = jnp.where(
        head_index == 0,
        jnp.concatenate([own_by_depth, other_by_depth], 1),
        jnp.concatenate([other_by_depth, own_by_depth], 1),
    )
    for chunk in (1, 0):
        span = slice(chunk * half_tokens, (chunk + 1) * half_tokens)
        query = projected[0][span].reshape(half_tokens, local_heads, HEAD_DIM)
        scores = jnp.einsum(
            "thd,shd->hts", query, keys, preferred_element_type=jnp.float32
        ) * HEAD_DIM ** (-0.5)
        weights = jax.nn.softmax(scores, axis=-1).astype(jnp.bfloat16)
        attended = jnp.einsum(
            "hts,shd->thd", weights, values, preferred_element_type=jnp.float32
        ).astype(jnp.bfloat16)
        attended = attended.reshape(half_tokens, local_heads * HEAD_DIM)
        other_attended = lax.ppermute(attended, "head", [(0, 1), (1, 0)])
        own_term = jnp.dot(attended, w_out[0], preferred_element_type=jnp.float32)
        other_term = jnp.dot(other_attended, other_w_out, preferred_element_type=jnp.float32)
        part = stream[span] + (
            own_term.astype(jnp.bfloat16).astype(jnp.float32)
            + other_term.astype(jnp.bfloat16).astype(jnp.float32)
        )
        normed = layer_norm(part, norm_gain[1], norm_bias[1]).astype(jnp.bfloat16)
        hidden = jax.nn.gelu(
            jnp.dot(normed, w_up[0], preferred_element_type=jnp.float32), approximate=True
        ).astype(jnp.bfloat16)
        partial_forward = jnp.dot(hidden, w_down[0], preferred_element_type=jnp.float32)
        if chunk == 0:
            sent_latent, partial_forward = lax.optimization_barrier(
                (sent_latent, partial_forward)
            )
        part = part + partner_sum(partial_forward)
        latent = layer_norm(part, norm_gain[2 * LAYERS], norm_bias[2 * LAYERS]).astype(jnp.bfloat16)
        if chunk == 1:
            sent_latent = latent
        else:
            own_latent = latent
    arrived_latent = from_behind(sent_latent, "tile", 1)
    later = (tile_index > 0).astype(jnp.float32)
    half_side = side // 2
    lower_piece, upper_piece = [
        lax.dot_general(
            latent, decode_by_depth, (((1,), (2,)), ((), ())),
            preferred_element_type=jnp.float32,
        ).astype(jnp.bfloat16)
        for latent in (own_latent, arrived_latent)
    ]
    shape = lower_piece.shape
    token_a = lax.broadcasted_iota(jnp.int32, shape, 0) // (side * side)
    inner = lax.broadcasted_iota(jnp.int32, shape, 2) // PATCH
    places = (token_a * PATCH + inner).astype(jnp.float32)
    lower_profile = profile_of(places)
    upper_profile = profile_of(places + HALF)
    numerator = (
        lower_piece.astype(jnp.float32) * lower_profile
        + upper_piece.astype(jnp.float32) * upper_profile
    )
    denominator = lower_profile + later * upper_profile
    blended = (numerator / denominator).astype(jnp.bfloat16)
    arranged = blended.reshape(half_side * side, WIN, cell_cols)
    arranged = jnp.swapaxes(arranged, 1, 2).reshape(half_side, side, PATCH, PATCH, WIN)
    return arranged.transpose(0, 2, 1, 3, 4).reshape(HALF, WIN, WIN)


def solution(mesh):
    return jax.shard_map(
        body,
        mesh=mesh,
        in_specs=(
            P("tile", None, None),
            P("tile", None),
            P(None, "head"),
            P(None, "head"),
            P(None, "head"),
            P(),
            P(),
            P(None, None, None, "head"),
            P(None, "head", None),
            P(None, None, "head"),
            P(None, "head", None),
            P(None, "head"),
        ),
        out_specs=P("tile", None, None),
        check_vma=False,
    )
```

```python
import jax
import jax.numpy as jnp
from jax import lax
from jax.sharding import PartitionSpec as P

PATCH = 16
LAYERS = 1
WIN = 128
HEAD_DIM = 64
HALF = 64


EPSILON = 1e-06


def from_behind(block, axis, distance):
    devices = range(lax.axis_size(axis))
    route = [(i - distance, i) for i in devices if i - distance in devices]
    return lax.ppermute(block, axis, route)


def partner_sum(term):
    rounded = term.astype(jnp.bfloat16)
    other = lax.ppermute(rounded, "head", [(0, 1), (1, 0)])
    return rounded.astype(jnp.float32) + other.astype(jnp.float32)


def layer_norm(values, gain, bias):
    average = jnp.mean(values, axis=-1, keepdims=True)
    centered = values - average
    variance = jnp.mean(centered * centered, axis=-1, keepdims=True)
    return centered * lax.rsqrt(variance + EPSILON) * gain + bias


def profile_of(places):
    return jnp.exp(-0.5 * ((places - (WIN - 1) / 2) / (WIN / 4)) ** 2)


def embed_planes(amplitudes, live, embed_by_depth, embed_mask):
    side = WIN // PATCH
    depth_side = amplitudes.shape[0] // PATCH
    rows = depth_side * side * side
    masked = amplitudes * live[:, :, None]
    grouped = masked.reshape(depth_side, PATCH, side, PATCH, WIN).transpose(0, 2, 1, 3, 4)
    grouped = grouped.reshape(depth_side * side, PATCH * PATCH, WIN)
    voxels = jnp.swapaxes(grouped, 1, 2).reshape(rows, PATCH, PATCH * PATCH)
    embedded = lax.dot_general(
        voxels, embed_by_depth, (((1, 2), (0, 1)), ((), ())),
        preferred_element_type=jnp.float32,
    )
    mask_patches = (
        live.reshape(depth_side, PATCH, side, PATCH)
        .transpose(0, 2, 1, 3)
        .reshape(depth_side * side, PATCH * PATCH)
    )
    mask_terms = jnp.dot(mask_patches, embed_mask, preferred_element_type=jnp.float32)
    local_width = mask_terms.shape[1]
    return embedded + jnp.broadcast_to(
        mask_terms[:, None, :], (depth_side * side, side, local_width)
    ).reshape(rows, local_width)


def body(
    traces,
    trace_mask,
    embed_voxel,
    embed_mask,
    position,
    norm_gain,
    norm_bias,
    w_qkv,
    w_out,
    w_up,
    w_down,
    w_decode,
):
    side = WIN // PATCH
    tokens = side**3
    half_tokens = tokens // 2
    tile_index = lax.axis_index("tile")
    head_index = lax.axis_index("head")
    own_live = trace_mask.astype(jnp.bfloat16)
    tile_count = lax.axis_size("tile")
    devices = 2 * tile_count
    across = [(index, index ^ (tile_count + 1)) for index in range(devices)]
    other_w_decode = lax.ppermute(w_decode, ("tile", "head"), across)
    other_w_out = lax.ppermute(w_out[0], ("tile", "head"), across)
    local_width = embed_voxel.shape[1]
    embed_by_depth = embed_voxel.reshape(PATCH * PATCH, PATCH, local_width).transpose(1, 0, 2)
    position = position.astype(jnp.float32)
    own_embedded = embed_planes(traces, own_live, embed_by_depth, embed_mask)
    own_half = (own_embedded + position[:half_tokens]).astype(jnp.bfloat16)
    for_previous = (own_embedded + position[half_tokens:]).astype(jnp.bfloat16)
    next_half = jnp.where(
        tile_index == lax.axis_size("tile") - 1,
        position[half_tokens:].astype(jnp.bfloat16),
        from_behind(for_previous, "tile", -1),
    )
    halves = []
    for embedded in (own_half, next_half):
        other_columns = lax.ppermute(embedded, "head", [(0, 1), (1, 0)])
        halves.append(jnp.where(
            head_index == 0,
            jnp.concatenate([embedded, other_columns], 1),
            jnp.concatenate([other_columns, embedded], 1),
        ).astype(jnp.float32))
    stream = jnp.concatenate(halves, 0)
    local_heads = w_qkv.shape[3] // HEAD_DIM
    normed = layer_norm(stream, norm_gain[0], norm_bias[0]).astype(jnp.bfloat16)
    projected = jnp.einsum(
        "td,sde->ste", normed, w_qkv[0], preferred_element_type=jnp.float32
    ).astype(jnp.bfloat16)
    keys = projected[1].reshape(tokens, local_heads, HEAD_DIM)
    values = projected[2].reshape(tokens, local_heads, HEAD_DIM)
    whole_w_decode = jnp.where(
        head_index == 0,
        jnp.concatenate([w_decode, other_w_decode], 1),
        jnp.concatenate([other_w_decode, w_decode], 1),
    )
    inner_rows = PATCH
    cell_cols = inner_rows * PATCH
    decode_by_depth = (
        whole_w_decode.T.reshape(inner_rows, PATCH, PATCH, -1)
        .transpose(2, 0, 1, 3)
        .reshape(PATCH, cell_cols, -1)
    )
    for chunk in (1, 0):
        span = slice(chunk * half_tokens, (chunk + 1) * half_tokens)
        query = projected[0][span].reshape(half_tokens, local_heads, HEAD_DIM)
        scores = jnp.einsum(
            "thd,shd->hts", query, keys, preferred_element_type=jnp.float32
        ) * HEAD_DIM ** (-0.5)
        weights = jax.nn.softmax(scores, axis=-1).astype(jnp.bfloat16)
        attended = jnp.einsum(
            "hts,shd->thd", weights, values, preferred_element_type=jnp.float32
        ).astype(jnp.bfloat16)
        attended = attended.reshape(half_tokens, local_heads * HEAD_DIM)
        other_attended = lax.ppermute(attended, "head", [(0, 1), (1, 0)])
        own_term = jnp.dot(attended, w_out[0], preferred_element_type=jnp.float32)
        other_term = jnp.dot(other_attended, other_w_out, preferred_element_type=jnp.float32)
        part = stream[span] + (
            own_term.astype(jnp.bfloat16).astype(jnp.float32)
            + other_term.astype(jnp.bfloat16).astype(jnp.float32)
        )
        normed = layer_norm(part, norm_gain[1], norm_bias[1]).astype(jnp.bfloat16)
        hidden = jax.nn.gelu(
            jnp.dot(normed, w_up[0], preferred_element_type=jnp.float32), approximate=True
        ).astype(jnp.bfloat16)
        partial_forward = jnp.dot(hidden, w_down[0], preferred_element_type=jnp.float32)
        if chunk == 0:
            sent_latent, partial_forward = lax.optimization_barrier(
                (sent_latent, partial_forward)
            )
        part = part + partner_sum(partial_forward)
        latent = layer_norm(part, norm_gain[2 * LAYERS], norm_bias[2 * LAYERS]).astype(jnp.bfloat16)
        if chunk == 1:
            sent_latent = latent
        else:
            own_latent = latent
    arrived_latent = from_behind(sent_latent, "tile", 1)
    later = (tile_index > 0).astype(jnp.float32)
    half_side = side // 2
    lower_piece, upper_piece = [
        lax.dot_general(
            latent, decode_by_depth, (((1,), (2,)), ((), ())),
            preferred_element_type=jnp.float32,
        ).astype(jnp.bfloat16)
        for latent in (own_latent, arrived_latent)
    ]
    shape = lower_piece.shape
    token_a = lax.broadcasted_iota(jnp.int32, shape, 0) // (side * side)
    inner = lax.broadcasted_iota(jnp.int32, shape, 2) // PATCH
    places = (token_a * PATCH + inner).astype(jnp.float32)
    lower_profile = profile_of(places)
    upper_profile = profile_of(places + HALF)
    numerator = (
        lower_piece.astype(jnp.float32) * lower_profile
        + upper_piece.astype(jnp.float32) * upper_profile
    )
    denominator = lower_profile + later * upper_profile
    blended = (numerator / denominator).astype(jnp.bfloat16)
    arranged = blended.reshape(half_side * side, WIN, cell_cols)
    arranged = jnp.swapaxes(arranged, 1, 2).reshape(half_side, side, PATCH, PATCH, WIN)
    return arranged.transpose(0, 2, 1, 3, 4).reshape(HALF, WIN, WIN)


def solution(mesh):
    return jax.shard_map(
        body,
        mesh=mesh,
        in_specs=(
            P("tile", None, None),
            P("tile", None),
            P(None, "head"),
            P(None, "head"),
            P(None, "head"),
            P(),
            P(),
            P(None, None, None, "head"),
            P(None, "head", None),
            P(None, None, "head"),
            P(None, "head", None),
            P(None, "head"),
        ),
        out_specs=P("tile", None, None),
        check_vma=False,
    )
```

```python
import jax
import jax.numpy as jnp
from jax import lax
from jax.sharding import PartitionSpec as P

PATCH = 16
LAYERS = 1
WIN = 128
HEAD_DIM = 64
HALF = 64


EPSILON = 1e-06


def from_behind(block, axis, distance):
    devices = range(lax.axis_size(axis))
    route = [(i - distance, i) for i in devices if i - distance in devices]
    return lax.ppermute(block, axis, route)


def partner_sum(term):
    rounded = term.astype(jnp.bfloat16)
    other = lax.ppermute(rounded, "head", [(0, 1), (1, 0)])
    return rounded.astype(jnp.float32) + other.astype(jnp.float32)


def layer_norm(values, gain, bias):
    average = jnp.mean(values, axis=-1, keepdims=True)
    centered = values - average
    variance = jnp.mean(centered * centered, axis=-1, keepdims=True)
    return centered * lax.rsqrt(variance + EPSILON) * gain + bias


def profile_of(places):
    return jnp.exp(-0.5 * ((places - (WIN - 1) / 2) / (WIN / 4)) ** 2)


def embed_planes(amplitudes, live, embed_by_depth, embed_mask):
    side = WIN // PATCH
    depth_side = amplitudes.shape[0] // PATCH
    rows = depth_side * side * side
    masked = amplitudes * live[:, :, None]
    grouped = masked.reshape(depth_side, PATCH, side, PATCH, WIN).transpose(0, 2, 1, 3, 4)
    grouped = grouped.reshape(depth_side * side, PATCH * PATCH, WIN)
    voxels = jnp.swapaxes(grouped, 1, 2).reshape(rows, PATCH, PATCH * PATCH)
    embedded = lax.dot_general(
        voxels, embed_by_depth, (((1, 2), (0, 1)), ((), ())),
        preferred_element_type=jnp.float32,
    )
    mask_patches = (
        live.reshape(depth_side, PATCH, side, PATCH)
        .transpose(0, 2, 1, 3)
        .reshape(depth_side * side, PATCH * PATCH)
    )
    mask_terms = jnp.dot(mask_patches, embed_mask, preferred_element_type=jnp.float32)
    local_width = mask_terms.shape[1]
    return embedded + jnp.broadcast_to(
        mask_terms[:, None, :], (depth_side * side, side, local_width)
    ).reshape(rows, local_width)


def body(
    traces,
    trace_mask,
    embed_voxel,
    embed_mask,
    position,
    norm_gain,
    norm_bias,
    w_qkv,
    w_out,
    w_up,
    w_down,
    w_decode,
):
    side = WIN // PATCH
    tokens = side**3
    half_tokens = tokens // 2
    tile_index = lax.axis_index("tile")
    head_index = lax.axis_index("head")
    own_live = trace_mask.astype(jnp.bfloat16)
    tile_count = lax.axis_size("tile")
    devices = 2 * tile_count
    across = [(index, index ^ (tile_count + 1)) for index in range(devices)]
    other_w_decode = lax.ppermute(w_decode, ("tile", "head"), across)
    other_w_out = lax.ppermute(w_out[0], "head", [(0, 1), (1, 0)])
    local_width = embed_voxel.shape[1]
    embed_by_depth = embed_voxel.reshape(PATCH * PATCH, PATCH, local_width).transpose(1, 0, 2)
    position = position.astype(jnp.float32)
    own_embedded = embed_planes(traces, own_live, embed_by_depth, embed_mask)
    own_half = (own_embedded + position[:half_tokens]).astype(jnp.bfloat16)
    for_previous = (own_embedded + position[half_tokens:]).astype(jnp.bfloat16)
    next_half = jnp.where(
        tile_index == lax.axis_size("tile") - 1,
        position[half_tokens:].astype(jnp.bfloat16),
        from_behind(for_previous, "tile", -1),
    )
    halves = []
    for embedded in (own_half, next_half):
        other_columns = lax.ppermute(embedded, "head", [(0, 1), (1, 0)])
        halves.append(jnp.where(
            head_index == 0,
            jnp.concatenate([embedded, other_columns], 1),
            jnp.concatenate([other_columns, embedded], 1),
        ).astype(jnp.float32))
    stream = jnp.concatenate(halves, 0)
    local_heads = w_qkv.shape[3] // HEAD_DIM
    normed = layer_norm(stream, norm_gain[0], norm_bias[0]).astype(jnp.bfloat16)
    projected = jnp.einsum(
        "td,sde->ste", normed, w_qkv[0], preferred_element_type=jnp.float32
    ).astype(jnp.bfloat16)
    keys = projected[1].reshape(tokens, local_heads, HEAD_DIM)
    values = projected[2].reshape(tokens, local_heads, HEAD_DIM)
    local_columns = w_decode.shape[1]
    whole_w_decode = lax.dynamic_slice_in_dim(
        jnp.concatenate([w_decode, other_w_decode, w_decode], 1),
        head_index * local_columns, 2 * local_columns, 1,
    )
    inner_rows = PATCH
    cell_cols = inner_rows * PATCH
    decode_by_depth = (
        whole_w_decode.T.reshape(inner_rows, PATCH, PATCH, -1)
        .transpose(2, 0, 1, 3)
        .reshape(PATCH, cell_cols, -1)
    )
    for chunk in (1, 0):
        span = slice(chunk * half_tokens, (chunk + 1) * half_tokens)
        query = projected[0][span].reshape(half_tokens, local_heads, HEAD_DIM)
        scores = jnp.einsum(
            "thd,shd->hts", query, keys, preferred_element_type=jnp.float32
        ) * HEAD_DIM ** (-0.5)
        weights = jax.nn.softmax(scores, axis=-1).astype(jnp.bfloat16)
        attended = jnp.einsum(
            "hts,shd->thd", weights, values, preferred_element_type=jnp.float32
        ).astype(jnp.bfloat16)
        attended = attended.reshape(half_tokens, local_heads * HEAD_DIM)
        other_attended = lax.ppermute(attended, "head", [(0, 1), (1, 0)])
        own_term = jnp.dot(attended, w_out[0], preferred_element_type=jnp.float32)
        other_term = jnp.dot(other_attended, other_w_out, preferred_element_type=jnp.float32)
        part = stream[span] + (
            own_term.astype(jnp.bfloat16).astype(jnp.float32)
            + other_term.astype(jnp.bfloat16).astype(jnp.float32)
        )
        normed = layer_norm(part, norm_gain[1], norm_bias[1]).astype(jnp.bfloat16)
        hidden = jax.nn.gelu(
            jnp.dot(normed, w_up[0], preferred_element_type=jnp.float32), approximate=True
        ).astype(jnp.bfloat16)
        partial_forward = jnp.dot(hidden, w_down[0], preferred_element_type=jnp.float32)
        if chunk == 0:
            sent_latent, partial_forward = lax.optimization_barrier(
                (sent_latent, partial_forward)
            )
        part = part + partner_sum(partial_forward)
        latent = layer_norm(part, norm_gain[2 * LAYERS], norm_bias[2 * LAYERS]).astype(jnp.bfloat16)
        if chunk == 1:
            sent_latent = latent
        else:
            own_latent = latent
    arrived_latent = from_behind(sent_latent, "tile", 1)
    later = (tile_index > 0).astype(jnp.float32)
    half_side = side // 2
    lower_piece, upper_piece = [
        lax.dot_general(
            latent, decode_by_depth, (((1,), (2,)), ((), ())),
            preferred_element_type=jnp.float32,
        ).astype(jnp.bfloat16)
        for latent in (own_latent, arrived_latent)
    ]
    shape = lower_piece.shape
    token_a = lax.broadcasted_iota(jnp.int32, shape, 0) // (side * side)
    inner = lax.broadcasted_iota(jnp.int32, shape, 2) // PATCH
    places = (token_a * PATCH + inner).astype(jnp.float32)
    lower_profile = profile_of(places)
    upper_profile = profile_of(places + HALF)
    numerator = (
        lower_piece.astype(jnp.float32) * lower_profile
        + upper_piece.astype(jnp.float32) * upper_profile
    )
    denominator = lower_profile + later * upper_profile
    blended = (numerator / denominator).astype(jnp.bfloat16)
    arranged = blended.reshape(half_side * side, WIN, cell_cols)
    arranged = jnp.swapaxes(arranged, 1, 2).reshape(half_side, side, PATCH, PATCH, WIN)
    return arranged.transpose(0, 2, 1, 3, 4).reshape(HALF, WIN, WIN)


def solution(mesh):
    return jax.shard_map(
        body,
        mesh=mesh,
        in_specs=(
            P("tile", None, None),
            P("tile", None),
            P(None, "head"),
            P(None, "head"),
            P(None, "head"),
            P(),
            P(),
            P(None, None, None, "head"),
            P(None, "head", None),
            P(None, None, "head"),
            P(None, "head", None),
            P(None, "head"),
        ),
        out_specs=P("tile", None, None),
        check_vma=False,
    )
```

```python
import jax
import jax.numpy as jnp
from jax import lax
from jax.sharding import PartitionSpec as P

PATCH = 16
LAYERS = 1
WIN = 128
HEAD_DIM = 64
HALF = 64


EPSILON = 1e-06


def from_behind(block, axis, distance):
    devices = range(lax.axis_size(axis))
    route = [(i - distance, i) for i in devices if i - distance in devices]
    return lax.ppermute(block, axis, route)


def partner_sum(term):
    rounded = term.astype(jnp.bfloat16)
    other = lax.ppermute(rounded, "head", [(0, 1), (1, 0)])
    return rounded.astype(jnp.float32) + other.astype(jnp.float32)


def layer_norm(values, gain, bias):
    average = jnp.mean(values, axis=-1, keepdims=True)
    centered = values - average
    variance = jnp.mean(centered * centered, axis=-1, keepdims=True)
    return centered * lax.rsqrt(variance + EPSILON) * gain + bias


def profile_of(places):
    return jnp.exp(-0.5 * ((places - (WIN - 1) / 2) / (WIN / 4)) ** 2)


def embed_planes(amplitudes, live, embed_by_depth, embed_mask):
    side = WIN // PATCH
    depth_side = amplitudes.shape[0] // PATCH
    rows = depth_side * side * side
    masked = amplitudes * live[:, :, None]
    grouped = masked.reshape(depth_side, PATCH, side, PATCH, WIN).transpose(0, 2, 1, 3, 4)
    grouped = grouped.reshape(depth_side * side, PATCH * PATCH, WIN)
    voxels = jnp.swapaxes(grouped, 1, 2).reshape(rows, PATCH, PATCH * PATCH)
    embedded = lax.dot_general(
        voxels, embed_by_depth, (((1, 2), (0, 1)), ((), ())),
        preferred_element_type=jnp.float32,
    )
    mask_patches = (
        live.reshape(depth_side, PATCH, side, PATCH)
        .transpose(0, 2, 1, 3)
        .reshape(depth_side * side, PATCH * PATCH)
    )
    mask_terms = jnp.dot(mask_patches, embed_mask, preferred_element_type=jnp.float32)
    local_width = mask_terms.shape[1]
    return embedded + jnp.broadcast_to(
        mask_terms[:, None, :], (depth_side * side, side, local_width)
    ).reshape(rows, local_width)


def body(
    traces,
    trace_mask,
    embed_voxel,
    embed_mask,
    position,
    norm_gain,
    norm_bias,
    w_qkv,
    w_out,
    w_up,
    w_down,
    w_decode,
):
    side = WIN // PATCH
    tokens = side**3
    half_tokens = tokens // 2
    tile_index = lax.axis_index("tile")
    head_index = lax.axis_index("head")
    own_live = trace_mask.astype(jnp.bfloat16)
    tile_count = lax.axis_size("tile")
    devices = 2 * tile_count
    across = [(index, index ^ (tile_count + 1)) for index in range(devices)]
    own_cells_first = w_decode.T
    other_cells_first = lax.ppermute(own_cells_first, ("tile", "head"), across)
    other_w_out = lax.ppermute(w_out[0], "head", [(0, 1), (1, 0)])
    local_width = embed_voxel.shape[1]
    embed_by_depth = embed_voxel.reshape(PATCH * PATCH, PATCH, local_width).transpose(1, 0, 2)
    position = position.astype(jnp.float32)
    own_embedded = embed_planes(traces, own_live, embed_by_depth, embed_mask)
    own_half = (own_embedded + position[:half_tokens]).astype(jnp.bfloat16)
    for_previous = (own_embedded + position[half_tokens:]).astype(jnp.bfloat16)
    next_half = jnp.where(
        tile_index == lax.axis_size("tile") - 1,
        position[half_tokens:].astype(jnp.bfloat16),
        from_behind(for_previous, "tile", -1),
    )
    halves = []
    for embedded in (own_half, next_half):
        other_columns = lax.ppermute(embedded, "head", [(0, 1), (1, 0)])
        halves.append(jnp.where(
            head_index == 0,
            jnp.concatenate([embedded, other_columns], 1),
            jnp.concatenate([other_columns, embedded], 1),
        ).astype(jnp.float32))
    stream = jnp.concatenate(halves, 0)
    local_heads = w_qkv.shape[3] // HEAD_DIM
    normed = layer_norm(stream, norm_gain[0], norm_bias[0]).astype(jnp.bfloat16)
    projected = jnp.einsum(
        "td,sde->ste", normed, w_qkv[0], preferred_element_type=jnp.float32
    ).astype(jnp.bfloat16)
    keys = projected[1].reshape(tokens, local_heads, HEAD_DIM)
    values = projected[2].reshape(tokens, local_heads, HEAD_DIM)
    cells_first = jnp.where(
        head_index == 0,
        jnp.concatenate([own_cells_first, other_cells_first], 0),
        jnp.concatenate([other_cells_first, own_cells_first], 0),
    )
    inner_rows = PATCH
    cell_cols = inner_rows * PATCH
    decode_by_depth = (
        cells_first.reshape(inner_rows, PATCH, PATCH, -1)
        .transpose(2, 0, 1, 3)
        .reshape(PATCH, cell_cols, -1)
    )
    for chunk in (1, 0):
        span = slice(chunk * half_tokens, (chunk + 1) * half_tokens)
        query = projected[0][span].reshape(half_tokens, local_heads, HEAD_DIM)
        scores = jnp.einsum(
            "thd,shd->hts", query, keys, preferred_element_type=jnp.float32
        ) * HEAD_DIM ** (-0.5)
        weights = jax.nn.softmax(scores, axis=-1).astype(jnp.bfloat16)
        attended = jnp.einsum(
            "hts,shd->thd", weights, values, preferred_element_type=jnp.float32
        ).astype(jnp.bfloat16)
        attended = attended.reshape(half_tokens, local_heads * HEAD_DIM)
        other_attended = lax.ppermute(attended, "head", [(0, 1), (1, 0)])
        own_term = jnp.dot(attended, w_out[0], preferred_element_type=jnp.float32)
        other_term = jnp.dot(other_attended, other_w_out, preferred_element_type=jnp.float32)
        part = stream[span] + (
            own_term.astype(jnp.bfloat16).astype(jnp.float32)
            + other_term.astype(jnp.bfloat16).astype(jnp.float32)
        )
        normed = layer_norm(part, norm_gain[1], norm_bias[1]).astype(jnp.bfloat16)
        hidden = jax.nn.gelu(
            jnp.dot(normed, w_up[0], preferred_element_type=jnp.float32), approximate=True
        ).astype(jnp.bfloat16)
        partial_forward = jnp.dot(hidden, w_down[0], preferred_element_type=jnp.float32)
        if chunk == 0:
            sent_latent, partial_forward = lax.optimization_barrier(
                (sent_latent, partial_forward)
            )
        part = part + partner_sum(partial_forward)
        latent = layer_norm(part, norm_gain[2 * LAYERS], norm_bias[2 * LAYERS]).astype(jnp.bfloat16)
        if chunk == 1:
            sent_latent = latent
        else:
            own_latent = latent
    arrived_latent = from_behind(sent_latent, "tile", 1)
    later = (tile_index > 0).astype(jnp.float32)
    half_side = side // 2
    lower_piece, upper_piece = [
        lax.dot_general(
            latent, decode_by_depth, (((1,), (2,)), ((), ())),
            preferred_element_type=jnp.float32,
        ).astype(jnp.bfloat16)
        for latent in (own_latent, arrived_latent)
    ]
    shape = lower_piece.shape
    token_a = lax.broadcasted_iota(jnp.int32, shape, 0) // (side * side)
    inner = lax.broadcasted_iota(jnp.int32, shape, 2) // PATCH
    places = (token_a * PATCH + inner).astype(jnp.float32)
    lower_profile = profile_of(places)
    upper_profile = profile_of(places + HALF)
    numerator = (
        lower_piece.astype(jnp.float32) * lower_profile
        + upper_piece.astype(jnp.float32) * upper_profile
    )
    denominator = lower_profile + later * upper_profile
    blended = (numerator / denominator).astype(jnp.bfloat16)
    arranged = blended.reshape(half_side * side, WIN, cell_cols)
    arranged = jnp.swapaxes(arranged, 1, 2).reshape(half_side, side, PATCH, PATCH, WIN)
    return arranged.transpose(0, 2, 1, 3, 4).reshape(HALF, WIN, WIN)


def solution(mesh):
    return jax.shard_map(
        body,
        mesh=mesh,
        in_specs=(
            P("tile", None, None),
            P("tile", None),
            P(None, "head"),
            P(None, "head"),
            P(None, "head"),
            P(),
            P(),
            P(None, None, None, "head"),
            P(None, "head", None),
            P(None, None, "head"),
            P(None, "head", None),
            P(None, "head"),
        ),
        out_specs=P("tile", None, None),
        check_vma=False,
    )
```

```python
import jax
import jax.numpy as jnp
from jax import lax
from jax.sharding import PartitionSpec as P

PATCH = 16
LAYERS = 1
WIN = 128
HEAD_DIM = 64
HALF = 64


EPSILON = 1e-06


def from_behind(block, axis, distance):
    devices = range(lax.axis_size(axis))
    route = [(i - distance, i) for i in devices if i - distance in devices]
    return lax.ppermute(block, axis, route)


def partner_sum(term):
    rounded = term.astype(jnp.bfloat16)
    other = lax.ppermute(rounded, "head", [(0, 1), (1, 0)])
    return rounded.astype(jnp.float32) + other.astype(jnp.float32)


def layer_norm(values, gain, bias):
    average = jnp.mean(values, axis=-1, keepdims=True)
    centered = values - average
    variance = jnp.mean(centered * centered, axis=-1, keepdims=True)
    return centered * lax.rsqrt(variance + EPSILON) * gain + bias


def profile_of(places):
    return jnp.exp(-0.5 * ((places - (WIN - 1) / 2) / (WIN / 4)) ** 2)


def embed_planes(amplitudes, live, embed_by_depth, embed_mask):
    side = WIN // PATCH
    depth_side = amplitudes.shape[0] // PATCH
    rows = depth_side * side * side
    masked = amplitudes * live[:, :, None]
    grouped = masked.reshape(depth_side, PATCH, side, PATCH, WIN).transpose(0, 2, 1, 3, 4)
    grouped = grouped.reshape(depth_side * side, PATCH * PATCH, WIN)
    voxels = jnp.swapaxes(grouped, 1, 2).reshape(rows, PATCH, PATCH * PATCH)
    embedded = lax.dot_general(
        voxels, embed_by_depth, (((1, 2), (0, 1)), ((), ())),
        preferred_element_type=jnp.float32,
    )
    mask_patches = (
        live.reshape(depth_side, PATCH, side, PATCH)
        .transpose(0, 2, 1, 3)
        .reshape(depth_side * side, PATCH * PATCH)
    )
    mask_terms = jnp.dot(mask_patches, embed_mask, preferred_element_type=jnp.float32)
    local_width = mask_terms.shape[1]
    return embedded + jnp.broadcast_to(
        mask_terms[:, None, :], (depth_side * side, side, local_width)
    ).reshape(rows, local_width)


def body(
    traces,
    trace_mask,
    embed_voxel,
    embed_mask,
    position,
    norm_gain,
    norm_bias,
    w_qkv,
    w_out,
    w_up,
    w_down,
    w_decode,
):
    side = WIN // PATCH
    tokens = side**3
    half_tokens = tokens // 2
    tile_index = lax.axis_index("tile")
    head_index = lax.axis_index("head")
    own_live = trace_mask.astype(jnp.bfloat16)
    tile_count = lax.axis_size("tile")
    devices = 2 * tile_count
    across = [(index, index ^ (tile_count + 1)) for index in range(devices)]
    own_cells_first = w_decode.T
    other_cells_first = lax.ppermute(own_cells_first, ("tile", "head"), across)
    other_w_out = lax.ppermute(w_out[0], "head", [(0, 1), (1, 0)])
    local_width = embed_voxel.shape[1]
    embed_by_depth = embed_voxel.reshape(PATCH * PATCH, PATCH, local_width).transpose(1, 0, 2)
    position = position.astype(jnp.float32)
    own_embedded = embed_planes(traces, own_live, embed_by_depth, embed_mask)
    own_half = (own_embedded + position[:half_tokens]).astype(jnp.bfloat16)
    for_previous = (own_embedded + position[half_tokens:]).astype(jnp.bfloat16)
    next_half = jnp.where(
        tile_index == lax.axis_size("tile") - 1,
        position[half_tokens:].astype(jnp.bfloat16),
        from_behind(for_previous, "tile", -1),
    )
    halves = []
    for embedded in (own_half, next_half):
        other_columns = lax.ppermute(embedded, "head", [(0, 1), (1, 0)])
        halves.append(jnp.where(
            head_index == 0,
            jnp.concatenate([embedded, other_columns], 1),
            jnp.concatenate([other_columns, embedded], 1),
        ).astype(jnp.float32))
    stream = jnp.concatenate(halves, 0)
    local_heads = w_qkv.shape[3] // HEAD_DIM
    normed = layer_norm(stream, norm_gain[0], norm_bias[0]).astype(jnp.bfloat16)
    projected = jnp.einsum(
        "td,sde->ste", normed, w_qkv[0], preferred_element_type=jnp.float32
    ).astype(jnp.bfloat16)
    keys = projected[1].reshape(tokens, local_heads, HEAD_DIM)
    values = projected[2].reshape(tokens, local_heads, HEAD_DIM)
    cells_first = jnp.concatenate([own_cells_first, other_cells_first], 0)
    inner_rows = PATCH
    cell_cols = inner_rows * PATCH
    decode_by_depth = (
        cells_first.reshape(inner_rows, PATCH, PATCH, -1)
        .transpose(2, 0, 1, 3)
        .reshape(PATCH, cell_cols, -1)
    )
    for chunk in (1, 0):
        span = slice(chunk * half_tokens, (chunk + 1) * half_tokens)
        query = projected[0][span].reshape(half_tokens, local_heads, HEAD_DIM)
        scores = jnp.einsum(
            "thd,shd->hts", query, keys, preferred_element_type=jnp.float32
        ) * HEAD_DIM ** (-0.5)
        weights = jax.nn.softmax(scores, axis=-1).astype(jnp.bfloat16)
        attended = jnp.einsum(
            "hts,shd->thd", weights, values, preferred_element_type=jnp.float32
        ).astype(jnp.bfloat16)
        attended = attended.reshape(half_tokens, local_heads * HEAD_DIM)
        other_attended = lax.ppermute(attended, "head", [(0, 1), (1, 0)])
        own_term = jnp.dot(attended, w_out[0], preferred_element_type=jnp.float32)
        other_term = jnp.dot(other_attended, other_w_out, preferred_element_type=jnp.float32)
        part = stream[span] + (
            own_term.astype(jnp.bfloat16).astype(jnp.float32)
            + other_term.astype(jnp.bfloat16).astype(jnp.float32)
        )
        normed = layer_norm(part, norm_gain[1], norm_bias[1]).astype(jnp.bfloat16)
        hidden = jax.nn.gelu(
            jnp.dot(normed, w_up[0], preferred_element_type=jnp.float32), approximate=True
        ).astype(jnp.bfloat16)
        partial_forward = jnp.dot(hidden, w_down[0], preferred_element_type=jnp.float32)
        if chunk == 0:
            sent_latent, partial_forward = lax.optimization_barrier(
                (sent_latent, partial_forward)
            )
        part = part + partner_sum(partial_forward)
        latent = layer_norm(part, norm_gain[2 * LAYERS], norm_bias[2 * LAYERS]).astype(jnp.bfloat16)
        if chunk == 1:
            sent_latent = latent
        else:
            own_latent = latent
    arrived_latent = from_behind(sent_latent, "tile", 1)
    later = (tile_index > 0).astype(jnp.float32)
    half_side = side // 2
    lower_piece, upper_piece = [
        lax.dot_general(
            latent, decode_by_depth, (((1,), (2,)), ((), ())),
            preferred_element_type=jnp.float32,
        ).astype(jnp.bfloat16)
        for latent in (own_latent, arrived_latent)
    ]
    shape = lower_piece.shape
    token_a = lax.broadcasted_iota(jnp.int32, shape, 0) // (side * side)
    columns = lax.broadcasted_iota(jnp.int32, shape, 2)
    half_rows = PATCH // 2
    block = columns // (half_rows * PATCH)
    true_block = block + head_index - 2 * block * head_index
    inner = true_block * half_rows + (columns // PATCH) % half_rows
    places = (token_a * PATCH + inner).astype(jnp.float32)
    lower_profile = profile_of(places)
    upper_profile = profile_of(places + HALF)
    numerator = (
        lower_piece.astype(jnp.float32) * lower_profile
        + upper_piece.astype(jnp.float32) * upper_profile
    )
    denominator = lower_profile + later * upper_profile
    blended = (numerator / denominator).astype(jnp.bfloat16)
    arranged = blended.reshape(half_side * side, WIN, cell_cols)
    arranged = jnp.swapaxes(arranged, 1, 2).reshape(half_side, side, 2, PATCH // 2, PATCH, WIN)
    arranged = jnp.where(head_index == 0, arranged, arranged[:, :, ::-1])
    arranged = arranged.reshape(half_side, side, PATCH, PATCH, WIN)
    return arranged.transpose(0, 2, 1, 3, 4).reshape(HALF, WIN, WIN)


def solution(mesh):
    return jax.shard_map(
        body,
        mesh=mesh,
        in_specs=(
            P("tile", None, None),
            P("tile", None),
            P(None, "head"),
            P(None, "head"),
            P(None, "head"),
            P(),
            P(),
            P(None, None, None, "head"),
            P(None, "head", None),
            P(None, None, "head"),
            P(None, "head", None),
            P(None, "head"),
        ),
        out_specs=P("tile", None, None),
        check_vma=False,
    )
```

```python
import jax
import jax.numpy as jnp
from jax import lax
from jax.sharding import PartitionSpec as P

PATCH = 16
LAYERS = 1
WIN = 128
HEAD_DIM = 64
HALF = 64


EPSILON = 1e-06


def from_behind(block, axis, distance):
    devices = range(lax.axis_size(axis))
    route = [(i - distance, i) for i in devices if i - distance in devices]
    return lax.ppermute(block, axis, route)


def partner_sum(term):
    rounded = term.astype(jnp.bfloat16)
    other = lax.ppermute(rounded, "head", [(0, 1), (1, 0)])
    return rounded.astype(jnp.float32) + other.astype(jnp.float32)


def layer_norm(values, gain, bias):
    average = jnp.mean(values, axis=-1, keepdims=True)
    centered = values - average
    variance = jnp.mean(centered * centered, axis=-1, keepdims=True)
    return centered * lax.rsqrt(variance + EPSILON) * gain + bias


def profile_of(places):
    return jnp.exp(-0.5 * ((places - (WIN - 1) / 2) / (WIN / 4)) ** 2)


def embed_planes(amplitudes, live, embed_by_depth, embed_mask):
    side = WIN // PATCH
    depth_side = amplitudes.shape[0] // PATCH
    rows = depth_side * side * side
    masked = amplitudes * live[:, :, None]
    grouped = masked.reshape(depth_side, PATCH, side, PATCH, WIN).transpose(0, 2, 1, 3, 4)
    grouped = grouped.reshape(depth_side * side, PATCH * PATCH, WIN)
    voxels = jnp.swapaxes(grouped, 1, 2).reshape(rows, PATCH, PATCH * PATCH)
    embedded = lax.dot_general(
        voxels, embed_by_depth, (((1, 2), (0, 1)), ((), ())),
        preferred_element_type=jnp.float32,
    )
    mask_patches = (
        live.reshape(depth_side, PATCH, side, PATCH)
        .transpose(0, 2, 1, 3)
        .reshape(depth_side * side, PATCH * PATCH)
    )
    mask_terms = jnp.dot(mask_patches, embed_mask, preferred_element_type=jnp.float32)
    local_width = mask_terms.shape[1]
    return embedded + jnp.broadcast_to(
        mask_terms[:, None, :], (depth_side * side, side, local_width)
    ).reshape(rows, local_width)


def body(
    traces,
    trace_mask,
    embed_voxel,
    embed_mask,
    position,
    norm_gain,
    norm_bias,
    w_qkv,
    w_out,
    w_up,
    w_down,
    w_decode,
):
    side = WIN // PATCH
    tokens = side**3
    half_tokens = tokens // 2
    tile_index = lax.axis_index("tile")
    head_index = lax.axis_index("head")
    own_live = trace_mask.astype(jnp.bfloat16)
    tile_count = lax.axis_size("tile")
    devices = 2 * tile_count
    across = [(index, index ^ (tile_count + 1)) for index in range(devices)]
    own_cells_first = w_decode.T
    other_cells_first = lax.ppermute(own_cells_first, ("tile", "head"), across)
    other_w_out = lax.ppermute(w_out[0], "head", [(0, 1), (1, 0)])
    local_width = embed_voxel.shape[1]
    embed_by_depth = embed_voxel.reshape(PATCH * PATCH, PATCH, local_width).transpose(1, 0, 2)
    position = position.astype(jnp.float32)
    own_embedded = embed_planes(traces, own_live, embed_by_depth, embed_mask)
    own_half = (own_embedded + position[:half_tokens]).astype(jnp.bfloat16)
    for_previous = (own_embedded + position[half_tokens:]).astype(jnp.bfloat16)
    last_tile = tile_index == lax.axis_size("tile") - 1
    upper_position = position[half_tokens:].astype(jnp.bfloat16)
    pair = [(0, 1), (1, 0)]
    diagonal = [
        ((tile + 1) * 2 + head, tile * 2 + 1 - head)
        for tile in range(lax.axis_size("tile") - 1)
        for head in range(2)
    ]
    next_own = jnp.where(last_tile, upper_position, from_behind(for_previous, "tile", -1))
    next_other = jnp.where(
        last_tile,
        lax.ppermute(upper_position, "head", pair),
        lax.ppermute(for_previous, ("tile", "head"), diagonal),
    )
    halves = []
    for embedded, other_columns in (
        (own_half, lax.ppermute(own_half, "head", pair)),
        (next_own, next_other),
    ):
        halves.append(jnp.where(
            head_index == 0,
            jnp.concatenate([embedded, other_columns], 1),
            jnp.concatenate([other_columns, embedded], 1),
        ).astype(jnp.float32))
    stream = jnp.concatenate(halves, 0)
    local_heads = w_qkv.shape[3] // HEAD_DIM
    normed = layer_norm(stream, norm_gain[0], norm_bias[0]).astype(jnp.bfloat16)
    projected = jnp.einsum(
        "td,sde->ste", normed, w_qkv[0], preferred_element_type=jnp.float32
    ).astype(jnp.bfloat16)
    keys = projected[1].reshape(tokens, local_heads, HEAD_DIM)
    values = projected[2].reshape(tokens, local_heads, HEAD_DIM)
    cells_first = jnp.where(
        head_index == 0,
        jnp.concatenate([own_cells_first, other_cells_first], 0),
        jnp.concatenate([other_cells_first, own_cells_first], 0),
    )
    inner_rows = PATCH
    cell_cols = inner_rows * PATCH
    decode_by_depth = (
        cells_first.reshape(inner_rows, PATCH, PATCH, -1)
        .transpose(2, 0, 1, 3)
        .reshape(PATCH, cell_cols, -1)
    )
    for chunk in (1, 0):
        span = slice(chunk * half_tokens, (chunk + 1) * half_tokens)
        query = projected[0][span].reshape(half_tokens, local_heads, HEAD_DIM)
        scores = jnp.einsum(
            "thd,shd->hts", query, keys, preferred_element_type=jnp.float32
        ) * HEAD_DIM ** (-0.5)
        weights = jax.nn.softmax(scores, axis=-1).astype(jnp.bfloat16)
        attended = jnp.einsum(
            "hts,shd->thd", weights, values, preferred_element_type=jnp.float32
        ).astype(jnp.bfloat16)
        attended = attended.reshape(half_tokens, local_heads * HEAD_DIM)
        other_attended = lax.ppermute(attended, "head", [(0, 1), (1, 0)])
        own_term = jnp.dot(attended, w_out[0], preferred_element_type=jnp.float32)
        other_term = jnp.dot(other_attended, other_w_out, preferred_element_type=jnp.float32)
        part = stream[span] + (
            own_term.astype(jnp.bfloat16).astype(jnp.float32)
            + other_term.astype(jnp.bfloat16).astype(jnp.float32)
        )
        normed = layer_norm(part, norm_gain[1], norm_bias[1]).astype(jnp.bfloat16)
        hidden = jax.nn.gelu(
            jnp.dot(normed, w_up[0], preferred_element_type=jnp.float32), approximate=True
        ).astype(jnp.bfloat16)
        partial_forward = jnp.dot(hidden, w_down[0], preferred_element_type=jnp.float32)
        if chunk == 0:
            sent_latent, partial_forward = lax.optimization_barrier(
                (sent_latent, partial_forward)
            )
        part = part + partner_sum(partial_forward)
        latent = layer_norm(part, norm_gain[2 * LAYERS], norm_bias[2 * LAYERS]).astype(jnp.bfloat16)
        if chunk == 1:
            sent_latent = latent
        else:
            own_latent = latent
    arrived_latent = from_behind(sent_latent, "tile", 1)
    later = (tile_index > 0).astype(jnp.float32)
    half_side = side // 2
    lower_piece, upper_piece = [
        lax.dot_general(
            latent, decode_by_depth, (((1,), (2,)), ((), ())),
            preferred_element_type=jnp.float32,
        ).astype(jnp.bfloat16)
        for latent in (own_latent, arrived_latent)
    ]
    shape = lower_piece.shape
    token_a = lax.broadcasted_iota(jnp.int32, shape, 0) // (side * side)
    inner = lax.broadcasted_iota(jnp.int32, shape, 2) // PATCH
    places = (token_a * PATCH + inner).astype(jnp.float32)
    lower_profile = profile_of(places)
    upper_profile = profile_of(places + HALF)
    numerator = (
        lower_piece.astype(jnp.float32) * lower_profile
        + upper_piece.astype(jnp.float32) * upper_profile
    )
    denominator = lower_profile + later * upper_profile
    blended = (numerator / denominator).astype(jnp.bfloat16)
    arranged = blended.reshape(half_side * side, WIN, cell_cols)
    arranged = jnp.swapaxes(arranged, 1, 2).reshape(half_side, side, PATCH, PATCH, WIN)
    return arranged.transpose(0, 2, 1, 3, 4).reshape(HALF, WIN, WIN)


def solution(mesh):
    return jax.shard_map(
        body,
        mesh=mesh,
        in_specs=(
            P("tile", None, None),
            P("tile", None),
            P(None, "head"),
            P(None, "head"),
            P(None, "head"),
            P(),
            P(),
            P(None, None, None, "head"),
            P(None, "head", None),
            P(None, None, "head"),
            P(None, "head", None),
            P(None, "head"),
        ),
        out_specs=P("tile", None, None),
        check_vma=False,
    )
```

```python
import jax
import jax.numpy as jnp
from jax import lax
from jax.sharding import PartitionSpec as P

PATCH = 16
LAYERS = 1
WIN = 128
HEAD_DIM = 64
HALF = 64


EPSILON = 1e-06


def from_behind(block, axis, distance):
    devices = range(lax.axis_size(axis))
    route = [(i - distance, i) for i in devices if i - distance in devices]
    return lax.ppermute(block, axis, route)


def partner_sum(term):
    rounded = term.astype(jnp.bfloat16)
    other = lax.ppermute(rounded, "head", [(0, 1), (1, 0)])
    return rounded.astype(jnp.float32) + other.astype(jnp.float32)


def layer_norm(values, gain, bias):
    average = jnp.mean(values, axis=-1, keepdims=True)
    centered = values - average
    variance = jnp.mean(centered * centered, axis=-1, keepdims=True)
    return centered * lax.rsqrt(variance + EPSILON) * gain + bias


def profile_of(places):
    return jnp.exp(-0.5 * ((places - (WIN - 1) / 2) / (WIN / 4)) ** 2)


def embed_planes(amplitudes, live, embed_by_depth, embed_mask):
    side = WIN // PATCH
    depth_side = amplitudes.shape[0] // PATCH
    rows = depth_side * side * side
    masked = amplitudes * live[:, :, None]
    grouped = masked.reshape(depth_side, PATCH, side, PATCH, WIN).transpose(0, 2, 1, 3, 4)
    grouped = grouped.reshape(depth_side * side, PATCH * PATCH, WIN)
    voxels = jnp.swapaxes(grouped, 1, 2).reshape(rows, PATCH, PATCH * PATCH)
    embedded = lax.dot_general(
        voxels, embed_by_depth, (((1, 2), (0, 1)), ((), ())),
        preferred_element_type=jnp.float32,
    )
    mask_patches = (
        live.reshape(depth_side, PATCH, side, PATCH)
        .transpose(0, 2, 1, 3)
        .reshape(depth_side * side, PATCH * PATCH)
    )
    mask_terms = jnp.dot(mask_patches, embed_mask, preferred_element_type=jnp.float32)
    local_width = mask_terms.shape[1]
    return embedded + jnp.broadcast_to(
        mask_terms[:, None, :], (depth_side * side, side, local_width)
    ).reshape(rows, local_width)


def body(
    traces,
    trace_mask,
    embed_voxel,
    embed_mask,
    position,
    norm_gain,
    norm_bias,
    w_qkv,
    w_out,
    w_up,
    w_down,
    w_decode,
):
    side = WIN // PATCH
    tokens = side**3
    half_tokens = tokens // 2
    tile_index = lax.axis_index("tile")
    head_index = lax.axis_index("head")
    own_live = trace_mask.astype(jnp.bfloat16)
    tile_count = lax.axis_size("tile")
    devices = 2 * tile_count
    across = [(index, index ^ (tile_count + 1)) for index in range(devices)]
    own_cells_first = w_decode.T
    other_cells_first = lax.ppermute(own_cells_first, ("tile", "head"), across)
    other_w_out = lax.ppermute(w_out[0], "head", [(0, 1), (1, 0)])
    local_width = embed_voxel.shape[1]
    embed_by_depth = embed_voxel.reshape(PATCH * PATCH, PATCH, local_width).transpose(1, 0, 2)
    position = position.astype(jnp.float32)
    own_embedded = embed_planes(traces, own_live, embed_by_depth, embed_mask)
    own_half = (own_embedded + position[:half_tokens]).astype(jnp.bfloat16)
    for_previous = (own_embedded + position[half_tokens:]).astype(jnp.bfloat16)
    next_half = jnp.where(
        tile_index == lax.axis_size("tile") - 1,
        position[half_tokens:].astype(jnp.bfloat16),
        from_behind(for_previous, "tile", -1),
    )
    halves = []
    for embedded in (own_half, next_half):
        other_columns = lax.ppermute(embedded, "head", [(0, 1), (1, 0)])
        halves.append(jnp.where(
            head_index == 0,
            jnp.concatenate([embedded, other_columns], 1),
            jnp.concatenate([other_columns, embedded], 1),
        ).astype(jnp.float32))
    stream = jnp.concatenate(halves, 0)
    local_heads = w_qkv.shape[3] // HEAD_DIM
    normed = layer_norm(stream, norm_gain[0], norm_bias[0]).astype(jnp.bfloat16)
    projected = jnp.einsum(
        "td,sde->ste", normed, w_qkv[0], preferred_element_type=jnp.float32
    ).astype(jnp.bfloat16)
    keys = projected[1].reshape(tokens, local_heads, HEAD_DIM)
    values = projected[2].reshape(tokens, local_heads, HEAD_DIM)
    cells_first = jnp.where(
        head_index == 0,
        jnp.concatenate([own_cells_first, other_cells_first], 0),
        jnp.concatenate([other_cells_first, own_cells_first], 0),
    )
    inner_rows = PATCH
    cell_cols = inner_rows * PATCH
    decode_by_depth = (
        cells_first.reshape(inner_rows, PATCH, PATCH, -1)
        .transpose(2, 0, 1, 3)
        .reshape(PATCH, cell_cols, -1)
    )
    for chunk in (1, 0):
        span = slice(chunk * half_tokens, (chunk + 1) * half_tokens)
        query = projected[0][span].reshape(half_tokens, local_heads, HEAD_DIM)
        scores = jnp.einsum(
            "thd,shd->hts", query, keys, preferred_element_type=jnp.float32
        ) * HEAD_DIM ** (-0.5)
        weights = jax.nn.softmax(scores, axis=-1).astype(jnp.bfloat16)
        attended = jnp.einsum(
            "hts,shd->thd", weights, values, preferred_element_type=jnp.float32
        ).astype(jnp.bfloat16)
        attended = attended.reshape(half_tokens, local_heads * HEAD_DIM)
        other_attended = lax.ppermute(attended, "head", [(0, 1), (1, 0)])
        own_term = jnp.dot(attended, w_out[0], preferred_element_type=jnp.float32)
        other_term = jnp.dot(other_attended, other_w_out, preferred_element_type=jnp.float32)
        part = stream[span] + (
            own_term.astype(jnp.bfloat16).astype(jnp.float32)
            + other_term.astype(jnp.bfloat16).astype(jnp.float32)
        )
        normed = layer_norm(part, norm_gain[1], norm_bias[1]).astype(jnp.bfloat16)
        hidden = jax.nn.gelu(
            jnp.dot(normed, w_up[0], preferred_element_type=jnp.float32), approximate=True
        ).astype(jnp.bfloat16)
        partial_forward = jnp.dot(hidden, w_down[0], preferred_element_type=jnp.float32)
        part = part + partner_sum(partial_forward)
        latent = layer_norm(part, norm_gain[2 * LAYERS], norm_bias[2 * LAYERS]).astype(jnp.bfloat16)
        if chunk == 1:
            sent_latent = latent
        else:
            own_latent = latent
    arrived_latent = from_behind(sent_latent, "tile", 1)
    later = (tile_index > 0).astype(jnp.float32)
    half_side = side // 2
    lower_piece, upper_piece = [
        lax.dot_general(
            latent, decode_by_depth, (((1,), (2,)), ((), ())),
            preferred_element_type=jnp.float32,
        ).astype(jnp.bfloat16)
        for latent in (own_latent, arrived_latent)
    ]
    shape = lower_piece.shape
    token_a = lax.broadcasted_iota(jnp.int32, shape, 0) // (side * side)
    inner = lax.broadcasted_iota(jnp.int32, shape, 2) // PATCH
    places = (token_a * PATCH + inner).astype(jnp.float32)
    lower_profile = profile_of(places)
    upper_profile = profile_of(places + HALF)
    numerator = (
        lower_piece.astype(jnp.float32) * lower_profile
        + upper_piece.astype(jnp.float32) * upper_profile
    )
    denominator = lower_profile + later * upper_profile
    blended = (numerator / denominator).astype(jnp.bfloat16)
    arranged = blended.reshape(half_side * side, WIN, cell_cols)
    arranged = jnp.swapaxes(arranged, 1, 2).reshape(half_side, side, PATCH, PATCH, WIN)
    return arranged.transpose(0, 2, 1, 3, 4).reshape(HALF, WIN, WIN)


def solution(mesh):
    return jax.shard_map(
        body,
        mesh=mesh,
        in_specs=(
            P("tile", None, None),
            P("tile", None),
            P(None, "head"),
            P(None, "head"),
            P(None, "head"),
            P(),
            P(),
            P(None, None, None, "head"),
            P(None, "head", None),
            P(None, None, "head"),
            P(None, "head", None),
            P(None, "head"),
        ),
        out_specs=P("tile", None, None),
        check_vma=False,
    )
```
